32 devices in a mesh: req: 4 (over z), exp: 8 (over y, x, core).
Axes of the slice: x: 2, y: 2, z: 4, core: 2. Of those that a mesh axis runs over, the one named last changes fastest.
Arguments:
- resid: bfloat16 [8192, 1536], P(('req', 'exp')), may hold values from -18 to 18
- queries: bfloat16 [8192, 1536], P(('req', 'exp')), may hold values from -40 to 40
- draft_kv: bfloat16 [8192, 1024], P(('req', 'exp')), may hold values from -6 to 6
- prompt_key_value: bfloat16 [16, 1024, 1024], P('exp', 'req'), may hold values from -6 to 6
- cache_page_store: bfloat16 [1536, 64, 1024], P(('req', 'exp')), may hold values from -6 to 6
- page_table: int32 [256, 6], P(('req', 'exp')), may hold values from 0 to 47, as said below
- cache_len: int32 [256], P(('req', 'exp')), may hold values from 1 to 384, as said below
- parents: int32 [256, 32], P(('req', 'exp')), may hold values from -1 to 30, as said below
- groups: int32 [256], P(('req', 'exp')), may hold values from 0 to 1
- w_out: bfloat16 [1536, 1536], replicated, may hold values from -0.15625 to 0.15625
- norm_gain: float32 [1536], replicated, may hold values from 0.25 to 1.75
- routes: int32 [8192, 8], P(('req', 'exp')), may hold values from 0 to 15, all different within a row; in each aligned block of 256 rows (0 to 255, 256 to 511, ...) at most 192 rows name the same one
- route_weight: float32 [8192, 8], P(('req', 'exp')), may hold values from 0.05 to 1
- w_in: bfloat16 [16, 1536, 1024], P('exp'), may hold values from -0.15625 to 0.15625
- w_down: bfloat16 [16, 512, 1536], P('exp'), may hold values from -0.25 to 0.25
Outputs:
- layer_out: bfloat16 [8192, 1536], P(('req', 'exp'))
The draws below stay inside these ranges and needn't reach their ends.
Inputs may be any that keep to these rules, and one draw needn't show every extreme that they name: `routes`: in each aligned block of 256 rows (the rows of one device) no expert is named by more than 192 rows, a bound that some block reaches; a row names 8 different experts. `page_table`: entries number the 48 pages held with the request's own block of 8 requests; slots past a request's cached positions are not read. `cache_len`: some request has exactly 384 cached positions. parents[r, 0] = -1 marks the root; for u > 0 the parent lies in 0 to u - 1.
All inputs are finite; a program needn't handle non-finite values.
Results may differ from the reference program's by a relative error of at most 0.01.
Values may be sent and summed in bfloat16 or wider, within the bound.
No kernel may reach another device: no remote copies, remote signals or barrier semaphores. Data moves between devices by JAX's collectives and lax.ppermute only.
A program may use at most 192 MiB of HBM per device.

```python
import math
import jax
import jax.numpy as jnp
import numpy as np
from jax import lax

D = 1536
QUERY_HEADS = 24
KEY_VALUE_HEADS = 8
HEAD_WIDTH = 64
FF = 512
TOPK = 8
TREE_TOKENS = 32
GROUPS_PER_COLUMN = 2
PAGE_POSITIONS = 64
MAXP = 6
R_DEV = 8
EXPERTS = 16
TOK_DEV = 256
REQUESTS = 256
DRAFT_TOKENS = 8192
PROMPT_POSITIONS = 1024
DEVICE_PAGES = 48
CAP = 192
N_EXP = 8
DEVICES = 32


def attention_pair(key):
    base = jax.random.fold_in(key, 11)
    first, second = jax.random.split(base, 2)
    key_value_width = KEY_VALUE_HEADS * HEAD_WIDTH
    query_draw = jnp.clip(jax.random.normal(first, (DRAFT_TOKENS, QUERY_HEADS * HEAD_WIDTH), jnp.float32) * 2.5, -15.0, 15.0)
    pair_draw = jnp.clip(jax.random.normal(second, (DRAFT_TOKENS, 2 * key_value_width), jnp.float32), -6.0, 6.0)
    return (query_draw, pair_draw)


def draw_queries(key, part):
    return attention_pair(key)[0].astype(jnp.bfloat16)


def draw_draft_kv(key, part):
    return attention_pair(key)[1].astype(jnp.bfloat16)


def draw_resid(key, part):
    first = jax.random.fold_in(jax.random.fold_in(key, 5), 0)
    value_matrix = jnp.clip(jax.random.normal(first, (DRAFT_TOKENS, D), jnp.float32), -6.0, 6.0)
    return value_matrix.astype(jnp.bfloat16)


def draw_page_table(key, part):
    block_total = REQUESTS // R_DEV
    block_keys = jax.random.split(jax.random.fold_in(key, 3), block_total)
    shuffled = jax.vmap(lambda block_key: jax.random.permutation(block_key, DEVICE_PAGES))(block_keys)
    return shuffled.reshape(REQUESTS, MAXP).astype(jnp.int32)


def draw_cache_len(key, part):
    first, second = jax.random.split(jax.random.fold_in(key, 17), 2)
    lengths = jax.random.randint(first, (REQUESTS,), 1, MAXP * PAGE_POSITIONS + 1, dtype=jnp.int32)
    fullest = jax.random.randint(second, (), 0, REQUESTS, dtype=jnp.int32)
    return lengths.at[fullest].set(MAXP * PAGE_POSITIONS)


def draw_parents(key, part):
    positions = jnp.arange(TREE_TOKENS, dtype=jnp.int32)
    upper = jnp.maximum(positions, 1)
    picked = jax.random.randint(jax.random.fold_in(key, 23), (REQUESTS, TREE_TOKENS), 0, upper[None, :], dtype=jnp.int32)
    return jnp.where(positions[None, :] == 0, -1, picked).astype(jnp.int32)


def plant(array, own_key, smallest, largest):
    extent = array.shape
    index_at = [jax.random.randint(jax.random.fold_in(own_key, axis), (), 0, extent[axis]) for axis in range(len(extent))]
    array = array.at[tuple(index_at)].set(smallest)
    longest = extent.index(max(extent))
    index_at[longest] = (index_at[longest] + 1) % extent[longest]
    return array.at[tuple(index_at)].set(largest)


def block_levels(key, shape, pieces, smallest, top_value):
    def one(axis_at, blocks):
        draws = jax.random.uniform(jax.random.fold_in(jax.random.fold_in(key, 6), axis_at), (blocks,), jnp.float32, smallest / len(pieces), top_value / len(pieces))
        return jnp.repeat(jnp.exp(draws), shape[axis_at] // blocks).reshape((-1,) + (1,) * (len(shape) - axis_at - 1))

    gain = one(*pieces[0])
    for cut in pieces[1:]:
        gain = gain * one(*cut)
    return gain


def routed_block(own_key, own, number, rows, amount, top, bound, lean):
    sequence = jax.random.permutation(own_key, amount)
    packed, common = portions_of(amount, rows * top, bound, lean, True), portions_of(amount, rows * top, bound, lean, False)
    places = jnp.arange(amount)

    def named(sizes, rotation):
        used = int((sizes > 0).sum())
        fixed = max(1, used // 4)
        moved = fixed + (places - fixed + rotation * (used - fixed)) % max(1, amount - fixed)
        return jnp.zeros((amount,), jnp.int32).at[sequence[jnp.where(places < fixed, places, moved)]].set(jnp.asarray(sizes, jnp.int32))

    sizes = jnp.where(number % 4 == 0, named(packed, number // 4), named(common, number - number // 4 - 1))
    mixed = jax.random.permutation(jax.random.fold_in(own, 3), amount)
    source_of, sink = mixed[0:amount // 2 * 2:2], mixed[1:amount // 2 * 2:2]
    slack = jnp.minimum(sizes[source_of] - 1, bound - sizes[sink]) // 2
    slack = jnp.where((source_of == sequence[0]) | (sink == sequence[0]) | (sizes[sink] == 0), 0, jnp.maximum(slack, 0))
    moved = jax.random.randint(jax.random.fold_in(own, 4), (amount // 2,), 0, 1 << 20) % (slack + 1)
    sizes = sizes.at[source_of].add(-moved).at[sink].add(moved)
    items = jnp.searchsorted(jnp.cumsum(sizes), jnp.arange(rows * top), side="right").astype(jnp.int32)
    table = items.reshape(top, rows).T
    table = table[jax.random.permutation(jax.random.fold_in(own, 1), rows)]
    rotation = jax.random.randint(jax.random.fold_in(own, 2), (rows, 1), 0, top)
    return jnp.take_along_axis(table, (jnp.arange(top)[None, :] + rotation) % top, axis=1)


def portions_of(number_of, total, most, lean, full):
    loads = [(1 << 20) // math.isqrt(standing ** lean) + 1 for standing in range(1, number_of + 1)]
    largest = most if full else min(most, max(-(-total // number_of), total * loads[0] // sum(loads)))
    least = 1 if total - largest >= number_of - 1 else 0
    given, spare = [largest] + [least] * (number_of - 1), total - largest - least * (number_of - 1)
    while spare > 0:
        candidates = [i for i in range(1, number_of) if given[i] < largest] or [i for i in range(1, number_of) if given[i] < most]
        mass, remaining = sum([loads[i] for i in candidates]), spare
        for i in candidates:
            extra = min(most - given[i], max(1, remaining * loads[i] // mass), spare)
            given[i] = given[i] + extra
            spare = spare - extra
    return np.array(given)


def noise(stream_key, shape, scale, most, cuts=(), kind=jnp.bfloat16):
    drawn = jax.random.normal(stream_key, shape, jnp.float32) * scale
    if len(cuts) > 0:
        drawn = block_levels(stream_key, shape, cuts, -0.22, 0.18) * drawn
    return jnp.clip(drawn, min=-most, max=most).astype(kind)


def setup_inputs(seed: int = 0) -> dict:
    splits = jax.random.split(jax.random.key(seed), 16)
    resid = draw_resid(jax.random.fold_in(splits[15], 71), 0)
    queries = draw_queries(jax.random.fold_in(splits[15], 71), 0)
    draft_kv = draw_draft_kv(jax.random.fold_in(splits[15], 71), 0)
    prompt_key_value = noise(splits[3], (GROUPS_PER_COLUMN * N_EXP, PROMPT_POSITIONS, 2 * KEY_VALUE_HEADS * HEAD_WIDTH), 1.0, 6.0, ((0, 8), (1, 4)))
    cache_page_store = noise(splits[4], (DEVICES * DEVICE_PAGES, PAGE_POSITIONS, 2 * KEY_VALUE_HEADS * HEAD_WIDTH), 1.0, 6.0, ((0, 32),))
    page_table = draw_page_table(jax.random.fold_in(splits[15], 71), 0)
    cache_len = draw_cache_len(jax.random.fold_in(splits[15], 71), 0)
    parents = draw_parents(jax.random.fold_in(splits[15], 71), 0)
    groups = plant(jax.random.randint(splits[8], (REQUESTS,), 0, GROUPS_PER_COLUMN), jax.random.fold_in(splits[8], 1), 0, GROUPS_PER_COLUMN - 1).astype(jnp.int32)
    w_out = noise(splits[9], (QUERY_HEADS * HEAD_WIDTH, D), (QUERY_HEADS * HEAD_WIDTH) ** -0.5, 0.15625)
    norm_gain = jnp.clip(1.0 + 0.15 * jax.random.normal(splits[10], (D,), jnp.float32), 0.25, 1.75)
    routes_keys = jax.random.split(jax.random.fold_in(splits[11], 1), DRAFT_TOKENS // TOK_DEV)
    routes_turns = jax.random.permutation(jax.random.fold_in(splits[11], 3), DRAFT_TOKENS // TOK_DEV)
    routes = jax.vmap(lambda own, number: routed_block(jax.random.fold_in(splits[11], 2), own, number, TOK_DEV, EXPERTS, TOPK, CAP, 1))(routes_keys, routes_turns).reshape((DRAFT_TOKENS, TOPK))
    route_weight = jnp.clip(jnp.exp(math.log(1.0) - 2.9957323 * jax.random.uniform(splits[12], (DRAFT_TOKENS, TOPK), jnp.float32) ** block_levels(splits[12], (DRAFT_TOKENS, TOPK), ((0, 32),), -0.2, 0.2)), 0.05, 1.0)
    w_in = noise(splits[13], (EXPERTS, D, 2 * FF), D ** -0.5, 0.15625, ((0, 8),))
    w_down = noise(splits[14], (EXPERTS, FF, D), FF ** -0.5, 0.25, ((0, 8),))
    return {"resid": resid, "queries": queries, "draft_kv": draft_kv, "prompt_key_value": prompt_key_value, "cache_page_store": cache_page_store, "page_table": page_table, "cache_len": cache_len, "parents": parents, "groups": groups, "w_out": w_out, "norm_gain": norm_gain, "routes": routes, "route_weight": route_weight, "w_in": w_in, "w_down": w_down}


def ancestry(parent_rows):
    positions = jnp.arange(TREE_TOKENS, dtype=jnp.int32)
    linked = (parent_rows[:, None] == positions[None, :]).astype(jnp.float32)
    reach = jnp.eye(TREE_TOKENS, dtype=jnp.float32) + linked
    for sweep in range((TREE_TOKENS - 1).bit_length()):
        reach = jnp.minimum(jnp.dot(reach, reach, precision=lax.Precision.HIGHEST), jnp.float32(1.0))
    return reach > 0.5

def reference(resid, queries, draft_kv, prompt_key_value, cache_page_store, page_table, cache_len, parents, groups, w_out, norm_gain, routes, route_weight, w_in, w_down):
    key_value_width = KEY_VALUE_HEADS * HEAD_WIDTH
    heads_repeated = QUERY_HEADS // KEY_VALUE_HEADS
    context_output = MAXP * PAGE_POSITIONS
    prompt_length = prompt_key_value.shape[1]
    scale_factor = HEAD_WIDTH ** (-0.5)

    def attend_request(request):
        block = request // R_DEV
        column = block % N_EXP
        prompt_row = (column * GROUPS_PER_COLUMN + groups[request]).astype(jnp.int32)
        prompt_rows = lax.dynamic_index_in_dim(prompt_key_value, prompt_row, 0, keepdims=False)
        page_ids = (block * DEVICE_PAGES + page_table[request]).astype(jnp.int32)
        cached_rows = cache_page_store[page_ids].reshape(context_output, 2 * key_value_width)
        tree_rows = lax.dynamic_slice_in_dim(draft_kv, (request * TREE_TOKENS).astype(jnp.int32), TREE_TOKENS, 0)
        every_row = jnp.concatenate([prompt_rows, cached_rows, tree_rows], 0).astype(jnp.float32)
        count_of_keys = every_row.shape[0]
        key_matrix = every_row[:, :key_value_width].reshape(count_of_keys, KEY_VALUE_HEADS, HEAD_WIDTH)
        value_matrix = every_row[:, key_value_width:].reshape(count_of_keys, KEY_VALUE_HEADS, HEAD_WIDTH)
        rows_of_queries = lax.dynamic_slice_in_dim(queries, (request * TREE_TOKENS).astype(jnp.int32), TREE_TOKENS, 0)
        rows_of_queries = rows_of_queries.astype(jnp.float32).reshape(TREE_TOKENS, KEY_VALUE_HEADS, heads_repeated, HEAD_WIDTH)
        scores = jnp.einsum('tkrd,lkd->tkrl', rows_of_queries, key_matrix, precision=lax.Precision.HIGHEST) * scale_factor
        cached_mask = jnp.arange(context_output, dtype=jnp.int32) < cache_len[request]
        visible = jnp.concatenate([jnp.ones((TREE_TOKENS, prompt_length), dtype=bool), jnp.broadcast_to(cached_mask[None, :], (TREE_TOKENS, context_output)), ancestry(parents[request])], 1)
        scores = jnp.where(visible[:, None, None, :], scores, -jnp.inf)
        peak = lax.optimization_barrier(jnp.max(scores, -1, keepdims=True))
        expd = jnp.exp(scores - peak)
        weights = lax.optimization_barrier(expd.astype(jnp.bfloat16)).astype(jnp.float32)
        numer = jnp.einsum('tkrl,lkd->tkrd', weights, value_matrix, precision=lax.Precision.HIGHEST)
        denom = lax.optimization_barrier(jnp.sum(expd, -1))
        return (numer / denom[..., None]).reshape(TREE_TOKENS, QUERY_HEADS * HEAD_WIDTH).astype(jnp.bfloat16)
    attended = lax.map(attend_request, jnp.arange(REQUESTS, dtype=jnp.int32)).reshape(DRAFT_TOKENS, QUERY_HEADS * HEAD_WIDTH)
    mixed = resid.astype(jnp.float32) + jnp.dot(attended, w_out, preferred_element_type=jnp.float32)
    spread = lax.optimization_barrier(jnp.mean(mixed * mixed, -1, keepdims=True))
    normed = (mixed * lax.rsqrt(spread + 1e-05) * norm_gain).astype(jnp.bfloat16)
    flat_experts = routes.reshape(-1).astype(jnp.int32)
    flat_weights = route_weight.reshape(-1)
    order = jnp.argsort(flat_experts, stable=True).astype(jnp.int32)
    counts = lax.optimization_barrier(jnp.sum((flat_experts[:, None] == jnp.arange(EXPERTS, dtype=jnp.int32)[None, :]).astype(jnp.int32), 0))
    starts = (jnp.cumsum(counts) - counts).astype(jnp.int32)
    block_rows = 1024
    order_padded = jnp.concatenate([order, jnp.zeros((block_rows,), jnp.int32)])

    def expert_step(expert, totals):
        inner = w_in[expert]
        outer = w_down[expert]
        block_total = (counts[expert] + block_rows - 1) // block_rows

        def block_step(block_number, running):
            base = (starts[expert] + block_number * block_rows).astype(jnp.int32)
            picked = lax.dynamic_slice_in_dim(order_padded, base, block_rows, 0)
            live = jnp.arange(block_rows, dtype=jnp.int32) + block_number * block_rows < counts[expert]
            source = (picked // TOPK).astype(jnp.int32)
            rows = normed[source]
            both = jnp.dot(rows, inner, preferred_element_type=jnp.float32)
            act = (jax.nn.silu(both[:, :FF]) * both[:, FF:]).astype(jnp.bfloat16)
            result = jnp.dot(act, outer, preferred_element_type=jnp.float32).astype(jnp.bfloat16)
            result = lax.optimization_barrier(result).astype(jnp.float32)
            scaled = jnp.where(live, flat_weights[picked], jnp.float32(0.0))
            return running.at[source].add(scaled[:, None] * result)
        return lax.fori_loop(0, block_total, block_step, totals)
    totals = lax.fori_loop(0, EXPERTS, expert_step, jnp.zeros((DRAFT_TOKENS, D), jnp.float32))
    return (mixed + totals).astype(jnp.bfloat16)
```

```python
import math

import jax
import jax.numpy as jnp
from jax import lax
from jax.sharding import PartitionSpec as P

D = 1536
QUERY_HEADS = 24
KEY_VALUE_HEADS = 8
HEAD_WIDTH = 64
FF = 512
TOPK = 8
TREE_TOKENS = 32
GROUPS_PER_COLUMN = 2
PAGE_POSITIONS = 64
MAXP = 6


def ancestry(parent_rows):
    tree_size = parent_rows.shape[1]
    positions = jnp.arange(tree_size, dtype=jnp.int32)
    linked = (parent_rows[:, :, None] == positions[None, None, :]).astype(jnp.float32)
    reach = jnp.eye(tree_size, dtype=jnp.float32)[None] + linked
    for sweep in range((tree_size - 1).bit_length()):
        reach = jnp.minimum(
            jnp.einsum("bij,bjk->bik", reach, reach, precision=lax.Precision.HIGHEST),
            jnp.float32(1.0),
        )
    return reach > 0.5


def prompt_scores(queries_per_request, request_groups, piece, scale_factor):
    key_value_width = KEY_VALUE_HEADS * HEAD_WIDTH
    position_extent = piece.shape[1]
    selected_entries = piece[request_groups]
    key_matrix = selected_entries[..., :key_value_width].reshape(
        selected_entries.shape[0], position_extent, KEY_VALUE_HEADS, HEAD_WIDTH
    )
    value_matrix = selected_entries[..., key_value_width:].reshape(
        selected_entries.shape[0], position_extent, KEY_VALUE_HEADS, HEAD_WIDTH
    )
    scores = (
        jnp.einsum(
            "btkrd,bpkd->btkrp", queries_per_request, key_matrix, preferred_element_type=jnp.float32
        )
        * scale_factor
    )
    return (scores, value_matrix, jnp.max(scores, -1))


def per_device(
    resid,
    queries,
    draft_kv,
    prompt_key_value,
    cache_page_store,
    page_table,
    cache_len,
    parents,
    groups,
    w_out,
    norm_gain,
    routes,
    route_weight,
    w_in,
    w_down,
):
    count_of_tokens = queries.shape[0]
    count_of_requests = page_table.shape[0]
    key_value_width = KEY_VALUE_HEADS * HEAD_WIDTH
    heads_repeated = QUERY_HEADS // KEY_VALUE_HEADS
    scale_factor = HEAD_WIDTH ** (-0.5)
    context_output = MAXP * PAGE_POSITIONS
    queries_per_head = queries.reshape(count_of_tokens, KEY_VALUE_HEADS, heads_repeated, HEAD_WIDTH)
    queries_per_request = queries_per_head.reshape(
        count_of_requests, TREE_TOKENS, KEY_VALUE_HEADS, heads_repeated, HEAD_WIDTH
    )
    pages = cache_page_store[page_table].reshape(
        count_of_requests, context_output, 2 * key_value_width
    )
    local_rows = jnp.concatenate(
        [pages, draft_kv.reshape(count_of_requests, TREE_TOKENS, 2 * key_value_width)], 1
    )
    local_keys = local_rows[..., :key_value_width].reshape(
        count_of_requests, context_output + TREE_TOKENS, KEY_VALUE_HEADS, HEAD_WIDTH
    )
    local_values = local_rows[..., key_value_width:].reshape(
        count_of_requests, context_output + TREE_TOKENS, KEY_VALUE_HEADS, HEAD_WIDTH
    )
    local_scores = (
        jnp.einsum(
            "btkrd,blkd->btkrl", queries_per_request, local_keys, preferred_element_type=jnp.float32
        )
        * scale_factor
    )
    cached = jnp.arange(context_output, dtype=jnp.int32)[None, :] < cache_len[:, None]
    visible = jnp.concatenate(
        [
            jnp.broadcast_to(cached[:, None, :], (count_of_requests, TREE_TOKENS, context_output)),
            ancestry(parents),
        ],
        2,
    )
    local_scores = jnp.where(visible[:, :, None, None, :], local_scores, -jnp.inf)
    local_maximum = jnp.max(local_scores, -1)
    expd = jnp.exp(local_scores - local_maximum[..., None])
    numer = jnp.einsum(
        "btkrl,blkd->btkrd",
        expd.astype(jnp.bfloat16),
        local_values,
        preferred_element_type=jnp.float32,
    )
    home_numer = numer.reshape(count_of_tokens, QUERY_HEADS * HEAD_WIDTH)
    home_denom = jnp.sum(expd, -1).reshape(count_of_tokens, QUERY_HEADS)
    start_carry = (
        local_maximum.reshape(count_of_tokens, KEY_VALUE_HEADS, heads_repeated),
        home_denom.reshape(count_of_tokens, KEY_VALUE_HEADS, heads_repeated),
        home_numer.reshape(count_of_tokens, KEY_VALUE_HEADS, heads_repeated, HEAD_WIDTH),
    )
    piece = lax.all_gather(prompt_key_value, "req", axis=1, tiled=True)
    position_extent = piece.shape[1]
    sub_span = math.gcd(position_extent, 256)
    sub_total = position_extent // sub_span
    portions = piece.reshape(GROUPS_PER_COLUMN, sub_total, sub_span, 2 * key_value_width).transpose(
        1, 0, 2, 3
    )

    def advance(state, portion):
        peak_old, denom_old, numer_old = state
        scores, value_matrix, peak_part = prompt_scores(
            queries_per_request, groups, portion, scale_factor
        )
        peak_new = jnp.maximum(
            peak_old, peak_part.reshape(count_of_tokens, KEY_VALUE_HEADS, heads_repeated)
        )
        expd = jnp.exp(
            scores
            - peak_new.reshape(count_of_requests, TREE_TOKENS, KEY_VALUE_HEADS, heads_repeated)[
                ..., None
            ]
        )
        decay = jnp.exp(peak_old - peak_new)
        fresh = jnp.einsum(
            "btkrp,bpkd->btkrd",
            expd.astype(jnp.bfloat16),
            value_matrix,
            preferred_element_type=jnp.float32,
        )
        numer = numer_old * decay[..., None] + fresh.reshape(
            count_of_tokens, KEY_VALUE_HEADS, heads_repeated, HEAD_WIDTH
        )
        denom = denom_old * decay + jnp.sum(expd, -1).reshape(
            count_of_tokens, KEY_VALUE_HEADS, heads_repeated
        )
        return ((peak_new, denom, numer), None)

    carry_out, unused = lax.scan(advance, start_carry, portions)
    final_peak, denom_all, numer_all = carry_out
    numerator = numer_all.reshape(count_of_tokens, QUERY_HEADS * HEAD_WIDTH)
    denominator = denom_all.reshape(count_of_tokens, QUERY_HEADS)
    attended = (
        (numerator.reshape(count_of_tokens, QUERY_HEADS, HEAD_WIDTH) / denominator[..., None])
        .reshape(count_of_tokens, QUERY_HEADS * HEAD_WIDTH)
        .astype(jnp.bfloat16)
    )
    mixed = resid.astype(jnp.float32) + jnp.dot(attended, w_out, preferred_element_type=jnp.float32)
    spread = jnp.mean(mixed * mixed, -1, keepdims=True)
    normed = (mixed * lax.rsqrt(spread + 1e-05) * norm_gain).astype(jnp.bfloat16)
    local_experts = w_in.shape[0]
    first_expert = lax.axis_index("exp") * local_experts
    gathered = lax.all_gather(normed, "exp", axis=0, tiled=True)
    gathered_routes = lax.all_gather(routes, "exp", axis=0, tiled=True)
    gathered_weights = lax.all_gather(route_weight, "exp", axis=0, tiled=True)
    expert_ids = first_expert + jnp.arange(local_experts, dtype=jnp.int32)
    gate = jnp.sum(
        jnp.where(
            gathered_routes[None, :, :] == expert_ids[:, None, None],
            gathered_weights[None, :, :],
            jnp.float32(0.0),
        ),
        -1,
    )
    both = jnp.einsum("td,edf->etf", gathered, w_in, preferred_element_type=jnp.float32)
    act = (jax.nn.silu(both[..., :FF]) * both[..., FF:]).astype(jnp.bfloat16)
    result = jnp.einsum("etf,efd->etd", act, w_down, preferred_element_type=jnp.float32).astype(
        jnp.bfloat16
    )
    partial = jnp.sum(gate[..., None] * result.astype(jnp.float32), 0)
    blended = lax.psum_scatter(
        partial.astype(jnp.bfloat16), "exp", scatter_dimension=0, tiled=True
    ).astype(jnp.float32)
    return (mixed + blended).astype(jnp.bfloat16)


def solution(mesh):
    in_specs = (
        P(("req", "exp"), None),
        P(("req", "exp"), None),
        P(("req", "exp"), None),
        P("exp", "req", None),
        P(("req", "exp"), None, None),
        P(("req", "exp"), None),
        P(("req", "exp")),
        P(("req", "exp"), None),
        P(("req", "exp")),
        P(),
        P(),
        P(("req", "exp"), None),
        P(("req", "exp"), None),
        P("exp", None, None),
        P("exp", None, None),
    )
    out_specs = P(("req", "exp"), None)
    return jax.shard_map(
        per_device, mesh=mesh, in_specs=in_specs, out_specs=out_specs, check_vma=False
    )
```

```python
import math

import jax
import jax.numpy as jnp
from jax import lax
from jax.experimental import pallas as pl
from jax.experimental.pallas import tpu as pltpu
from jax.sharding import PartitionSpec as P

D = 1536
QUERY_HEADS = 24
KEY_VALUE_HEADS = 8
HEAD_WIDTH = 64
FF = 512
TOPK = 8
TREE_TOKENS = 32
GROUPS_PER_COLUMN = 2
PAGE_POSITIONS = 64
MAXP = 6


def ancestry(parent_rows):
    tree_size = parent_rows.shape[1]
    positions = jnp.arange(tree_size, dtype=jnp.int32)
    linked = (parent_rows[:, :, None] == positions[None, None, :]).astype(jnp.float32)
    reach = jnp.eye(tree_size, dtype=jnp.float32)[None] + linked
    for sweep in range((tree_size - 1).bit_length()):
        reach = jnp.minimum(
            jnp.einsum("bij,bjk->bik", reach, reach, precision=lax.Precision.HIGHEST),
            jnp.float32(1.0),
        )
    return reach > 0.5


def attention_kernel(groups_ref, pages_ref, lengths_ref, queries_ref, tree_ref, visible_ref, prompt_ref, *rest):
    page_refs = rest[:MAXP]
    out_ref = rest[MAXP]
    request = pl.program_id(0)
    key_value_width = KEY_VALUE_HEADS * HEAD_WIDTH
    heads_repeated = QUERY_HEADS // KEY_VALUE_HEADS
    rows = heads_repeated * TREE_TOKENS
    scale_factor = HEAD_WIDTH ** (-0.5)
    tree_visible = jnp.concatenate([visible_ref[0]] * heads_repeated, 0) > 0.5
    positions = lax.broadcasted_iota(jnp.int32, (rows, MAXP * PAGE_POSITIONS), 1)
    cache_visible = positions < lengths_ref[request]
    contract = (((1,), (1,)), ((), ()))

    for kv in range(KEY_VALUE_HEADS):
        key_at = kv * HEAD_WIDTH
        value_at = key_value_width + kv * HEAD_WIDTH
        query_rows = jnp.concatenate(
            [
                queries_ref[:, (kv * heads_repeated + j) * HEAD_WIDTH : (kv * heads_repeated + j + 1) * HEAD_WIDTH]
                for j in range(heads_repeated)
            ],
            0,
        )
        prompt_keys = prompt_ref[0, :, key_at : key_at + HEAD_WIDTH]
        prompt_values = prompt_ref[0, :, value_at : value_at + HEAD_WIDTH]
        cache_keys = jnp.concatenate([p[0, :, key_at : key_at + HEAD_WIDTH] for p in page_refs], 0)
        cache_values = jnp.concatenate([p[0, :, value_at : value_at + HEAD_WIDTH] for p in page_refs], 0)
        tree_keys = tree_ref[:, key_at : key_at + HEAD_WIDTH]
        tree_values = tree_ref[:, value_at : value_at + HEAD_WIDTH]
        prompt_scores = lax.dot_general(query_rows, prompt_keys, contract, preferred_element_type=jnp.float32) * scale_factor
        cache_scores = lax.dot_general(query_rows, cache_keys, contract, preferred_element_type=jnp.float32) * scale_factor
        tree_scores = lax.dot_general(query_rows, tree_keys, contract, preferred_element_type=jnp.float32) * scale_factor
        cache_scores = jnp.where(cache_visible, cache_scores, -jnp.inf)
        tree_scores = jnp.where(tree_visible, tree_scores, -jnp.inf)
        peak = jnp.maximum(
            jnp.maximum(jnp.max(prompt_scores, -1, keepdims=True), jnp.max(cache_scores, -1, keepdims=True)),
            jnp.max(tree_scores, -1, keepdims=True),
        )
        prompt_exp = jnp.exp(prompt_scores - peak)
        cache_exp = jnp.exp(cache_scores - peak)
        tree_exp = jnp.exp(tree_scores - peak)
        denom = (
            jnp.sum(prompt_exp, -1, keepdims=True)
            + jnp.sum(cache_exp, -1, keepdims=True)
            + jnp.sum(tree_exp, -1, keepdims=True)
        )
        numer = (
            jnp.dot(prompt_exp.astype(jnp.bfloat16), prompt_values, preferred_element_type=jnp.float32)
            + jnp.dot(cache_exp.astype(jnp.bfloat16), cache_values, preferred_element_type=jnp.float32)
            + jnp.dot(tree_exp.astype(jnp.bfloat16), tree_values, preferred_element_type=jnp.float32)
        )
        result = (numer / denom).astype(jnp.bfloat16)
        for j in range(heads_repeated):
            head = kv * heads_repeated + j
            out_ref[:, head * HEAD_WIDTH : (head + 1) * HEAD_WIDTH] = result[j * TREE_TOKENS : (j + 1) * TREE_TOKENS]


def attend(queries, draft_kv, piece, cache_page_store, page_table, cache_len, parents, groups):
    count_of_tokens, width = queries.shape
    count_of_requests = page_table.shape[0]
    row_width = draft_kv.shape[1]
    store_pages = cache_page_store.shape[0]
    visible = ancestry(parents).astype(jnp.float32)
    flat_pages = jnp.clip(page_table.reshape(-1), 0, store_pages - 1).astype(jnp.int32)
    prompt_groups = jnp.clip(groups, 0, piece.shape[0] - 1).astype(jnp.int32)

    def page_spec(slot):
        return pl.BlockSpec(
            (1, PAGE_POSITIONS, row_width), lambda r, g, p, c: (p[r * MAXP + slot], 0, 0)
        )

    grid_spec = pltpu.PrefetchScalarGridSpec(
        num_scalar_prefetch=3,
        grid=(count_of_requests,),
        in_specs=[
            pl.BlockSpec((TREE_TOKENS, width), lambda r, g, p, c: (r, 0)),
            pl.BlockSpec((TREE_TOKENS, row_width), lambda r, g, p, c: (r, 0)),
            pl.BlockSpec((1, TREE_TOKENS, TREE_TOKENS), lambda r, g, p, c: (r, 0, 0)),
            pl.BlockSpec((1, piece.shape[1], row_width), lambda r, g, p, c: (g[r], 0, 0)),
        ]
        + [page_spec(slot) for slot in range(MAXP)],
        out_specs=pl.BlockSpec((TREE_TOKENS, width), lambda r, g, p, c: (r, 0)),
    )
    return pl.pallas_call(
        attention_kernel,
        grid_spec=grid_spec,
        out_shape=jax.ShapeDtypeStruct((count_of_tokens, width), jnp.bfloat16),
    )(prompt_groups, flat_pages, cache_len.astype(jnp.int32), queries, draft_kv, visible, piece, *([cache_page_store] * MAXP))


def per_device(
    resid,
    queries,
    draft_kv,
    prompt_key_value,
    cache_page_store,
    page_table,
    cache_len,
    parents,
    groups,
    w_out,
    norm_gain,
    routes,
    route_weight,
    w_in,
    w_down,
):
    piece = lax.all_gather(prompt_key_value, "req", axis=1, tiled=True)
    attended = attend(queries, draft_kv, piece, cache_page_store, page_table, cache_len, parents, groups)
    mixed = resid.astype(jnp.float32) + jnp.dot(attended, w_out, preferred_element_type=jnp.float32)
    spread = jnp.mean(mixed * mixed, -1, keepdims=True)
    normed = (mixed * lax.rsqrt(spread + 1e-05) * norm_gain).astype(jnp.bfloat16)
    local_experts = w_in.shape[0]
    first_expert = lax.axis_index("exp") * local_experts
    gathered = lax.all_gather(normed, "exp", axis=0, tiled=True)
    gathered_routes = lax.all_gather(routes, "exp", axis=0, tiled=True)
    gathered_weights = lax.all_gather(route_weight, "exp", axis=0, tiled=True)
    expert_ids = first_expert + jnp.arange(local_experts, dtype=jnp.int32)
    gate = jnp.sum(
        jnp.where(
            gathered_routes[None, :, :] == expert_ids[:, None, None],
            gathered_weights[None, :, :],
            jnp.float32(0.0),
        ),
        -1,
    )
    both = jnp.einsum("td,edf->etf", gathered, w_in, preferred_element_type=jnp.float32)
    act = (jax.nn.silu(both[..., :FF]) * both[..., FF:]).astype(jnp.bfloat16)
    result = jnp.einsum("etf,efd->etd", act, w_down, preferred_element_type=jnp.float32).astype(
        jnp.bfloat16
    )
    partial = jnp.sum(gate[..., None] * result.astype(jnp.float32), 0)
    blended = lax.psum_scatter(
        partial.astype(jnp.bfloat16), "exp", scatter_dimension=0, tiled=True
    ).astype(jnp.float32)
    return (mixed + blended).astype(jnp.bfloat16)


def solution(mesh):
    in_specs = (
        P(("req", "exp"), None),
        P(("req", "exp"), None),
        P(("req", "exp"), None),
        P("exp", "req", None),
        P(("req", "exp"), None, None),
        P(("req", "exp"), None),
        P(("req", "exp")),
        P(("req", "exp"), None),
        P(("req", "exp")),
        P(),
        P(),
        P(("req", "exp"), None),
        P(("req", "exp"), None),
        P("exp", None, None),
        P("exp", None, None),
    )
    out_specs = P(("req", "exp"), None)
    return jax.shard_map(
        per_device, mesh=mesh, in_specs=in_specs, out_specs=out_specs, check_vma=False
    )
```

```python
import math

import jax
import jax.numpy as jnp
from jax import lax
from jax.experimental import pallas as pl
from jax.experimental.pallas import tpu as pltpu
from jax.sharding import PartitionSpec as P

D = 1536
QUERY_HEADS = 24
KEY_VALUE_HEADS = 8
HEAD_WIDTH = 64
FF = 512
TOPK = 8
TREE_TOKENS = 32
GROUPS_PER_COLUMN = 2
PAGE_POSITIONS = 64
MAXP = 6


def ancestry(parent_rows):
    tree_size = parent_rows.shape[1]
    positions = jnp.arange(tree_size, dtype=jnp.int32)
    linked = (parent_rows[:, :, None] == positions[None, None, :]).astype(jnp.float32)
    reach = jnp.eye(tree_size, dtype=jnp.float32)[None] + linked
    for sweep in range((tree_size - 1).bit_length()):
        reach = jnp.minimum(
            jnp.einsum("bij,bjk->bik", reach, reach, precision=lax.Precision.HIGHEST),
            jnp.float32(1.0),
        )
    return reach > 0.5


def attention_kernel(groups_ref, pages_ref, lengths_ref, queries_ref, tree_ref, visible_ref, prompt_ref, *rest):
    page_refs = rest[:MAXP]
    out_ref = rest[MAXP]
    request = pl.program_id(0)
    key_value_width = KEY_VALUE_HEADS * HEAD_WIDTH
    heads_repeated = QUERY_HEADS // KEY_VALUE_HEADS
    rows = heads_repeated * TREE_TOKENS
    scale_factor = HEAD_WIDTH ** (-0.5)
    tree_visible = jnp.concatenate([visible_ref[0]] * heads_repeated, 0) > 0.5
    positions = lax.broadcasted_iota(jnp.int32, (rows, MAXP * PAGE_POSITIONS), 1)
    cache_visible = positions < lengths_ref[request]
    contract = (((1,), (1,)), ((), ()))

    for kv in range(KEY_VALUE_HEADS):
        key_at = kv * HEAD_WIDTH
        value_at = key_value_width + kv * HEAD_WIDTH
        query_rows = jnp.concatenate(
            [
                queries_ref[:, (kv * heads_repeated + j) * HEAD_WIDTH : (kv * heads_repeated + j + 1) * HEAD_WIDTH]
                for j in range(heads_repeated)
            ],
            0,
        )
        prompt_keys = prompt_ref[0, :, key_at : key_at + HEAD_WIDTH]
        prompt_values = prompt_ref[0, :, value_at : value_at + HEAD_WIDTH]
        cache_keys = jnp.concatenate([p[0, :, key_at : key_at + HEAD_WIDTH] for p in page_refs], 0)
        cache_values = jnp.concatenate([p[0, :, value_at : value_at + HEAD_WIDTH] for p in page_refs], 0)
        tree_keys = tree_ref[:, key_at : key_at + HEAD_WIDTH]
        tree_values = tree_ref[:, value_at : value_at + HEAD_WIDTH]
        prompt_scores = lax.dot_general(query_rows, prompt_keys, contract, preferred_element_type=jnp.float32) * scale_factor
        cache_scores = lax.dot_general(query_rows, cache_keys, contract, preferred_element_type=jnp.float32) * scale_factor
        tree_scores = lax.dot_general(query_rows, tree_keys, contract, preferred_element_type=jnp.float32) * scale_factor
        cache_scores = jnp.where(cache_visible, cache_scores, -jnp.inf)
        tree_scores = jnp.where(tree_visible, tree_scores, -jnp.inf)
        peak = jnp.maximum(
            jnp.maximum(jnp.max(prompt_scores, -1, keepdims=True), jnp.max(cache_scores, -1, keepdims=True)),
            jnp.max(tree_scores, -1, keepdims=True),
        )
        prompt_exp = jnp.exp(prompt_scores - peak)
        cache_exp = jnp.exp(cache_scores - peak)
        tree_exp = jnp.exp(tree_scores - peak)
        denom = (
            jnp.sum(prompt_exp, -1, keepdims=True)
            + jnp.sum(cache_exp, -1, keepdims=True)
            + jnp.sum(tree_exp, -1, keepdims=True)
        )
        numer = (
            jnp.dot(prompt_exp.astype(jnp.bfloat16), prompt_values, preferred_element_type=jnp.float32)
            + jnp.dot(cache_exp.astype(jnp.bfloat16), cache_values, preferred_element_type=jnp.float32)
            + jnp.dot(tree_exp.astype(jnp.bfloat16), tree_values, preferred_element_type=jnp.float32)
        )
        result = (numer / denom).astype(jnp.bfloat16)
        for j in range(heads_repeated):
            head = kv * heads_repeated + j
            out_ref[:, head * HEAD_WIDTH : (head + 1) * HEAD_WIDTH] = result[j * TREE_TOKENS : (j + 1) * TREE_TOKENS]


def attend(queries, draft_kv, piece, cache_page_store, page_table, cache_len, parents, groups):
    count_of_tokens, width = queries.shape
    count_of_requests = page_table.shape[0]
    row_width = draft_kv.shape[1]
    store_pages = cache_page_store.shape[0]
    visible = ancestry(parents).astype(jnp.float32)
    flat_pages = jnp.clip(page_table.reshape(-1), 0, store_pages - 1).astype(jnp.int32)
    prompt_groups = jnp.clip(groups, 0, piece.shape[0] - 1).astype(jnp.int32)

    def page_spec(slot):
        return pl.BlockSpec(
            (1, PAGE_POSITIONS, row_width), lambda r, g, p, c: (p[r * MAXP + slot], 0, 0)
        )

    grid_spec = pltpu.PrefetchScalarGridSpec(
        num_scalar_prefetch=3,
        grid=(count_of_requests,),
        in_specs=[
            pl.BlockSpec((TREE_TOKENS, width), lambda r, g, p, c: (r, 0)),
            pl.BlockSpec((TREE_TOKENS, row_width), lambda r, g, p, c: (r, 0)),
            pl.BlockSpec((1, TREE_TOKENS, TREE_TOKENS), lambda r, g, p, c: (r, 0, 0)),
            pl.BlockSpec((1, piece.shape[1], row_width), lambda r, g, p, c: (g[r], 0, 0)),
        ]
        + [page_spec(slot) for slot in range(MAXP)],
        out_specs=pl.BlockSpec((TREE_TOKENS, width), lambda r, g, p, c: (r, 0)),
    )
    return pl.pallas_call(
        attention_kernel,
        grid_spec=grid_spec,
        out_shape=jax.ShapeDtypeStruct((count_of_tokens, width), jnp.bfloat16),
    )(prompt_groups, flat_pages, cache_len.astype(jnp.int32), queries, draft_kv, visible, piece, *([cache_page_store] * MAXP))


def per_device(
    resid,
    queries,
    draft_kv,
    prompt_key_value,
    cache_page_store,
    page_table,
    cache_len,
    parents,
    groups,
    w_out,
    norm_gain,
    routes,
    route_weight,
    w_in,
    w_down,
):
    local_experts = w_in.shape[0]
    exp_devices = lax.axis_size("exp")
    experts_all = local_experts * exp_devices
    count_of_tokens = routes.shape[0]
    every_expert = jnp.arange(experts_all, dtype=jnp.int32)
    gate_local = jnp.sum(
        jnp.where(routes[:, :, None] == every_expert[None, None, :], route_weight[:, :, None], jnp.float32(0.0)),
        1,
    )
    gate_gathered = lax.all_gather(gate_local, "exp", axis=0, tiled=True)
    gate = lax.dynamic_slice_in_dim(gate_gathered, lax.axis_index("exp") * local_experts, local_experts, 1)
    gate = gate.reshape(exp_devices, count_of_tokens, local_experts)
    piece = lax.all_gather(prompt_key_value, "req", axis=1, tiled=True)
    gate, piece = lax.optimization_barrier((gate, piece))
    attended = attend(queries, draft_kv, piece, cache_page_store, page_table, cache_len, parents, groups)
    mixed = resid.astype(jnp.float32) + jnp.dot(attended, w_out, preferred_element_type=jnp.float32)
    spread = jnp.mean(mixed * mixed, -1, keepdims=True)
    normed = (mixed * lax.rsqrt(spread + 1e-05) * norm_gain).astype(jnp.bfloat16)
    chunks = 2 if count_of_tokens % 16 == 0 else 1
    span = count_of_tokens // chunks
    pieces = []
    for chunk in range(chunks):
        rows = normed[chunk * span : (chunk + 1) * span]
        gathered = lax.all_gather(rows, "exp", axis=0, tiled=True)
        chunk_gate = gate[:, chunk * span : (chunk + 1) * span].reshape(exp_devices * span, local_experts)
        both = jnp.einsum("td,edf->etf", gathered, w_in, preferred_element_type=jnp.float32)
        act = (jax.nn.silu(both[..., :FF]) * both[..., FF:]).astype(jnp.bfloat16)
        result = jnp.einsum("etf,efd->etd", act, w_down, preferred_element_type=jnp.float32).astype(
            jnp.bfloat16
        )
        partial = jnp.sum(jnp.transpose(chunk_gate)[..., None] * result.astype(jnp.float32), 0)
        pieces.append(
            lax.psum_scatter(partial.astype(jnp.bfloat16), "exp", scatter_dimension=0, tiled=True)
        )
    blended = jnp.concatenate(pieces, 0).astype(jnp.float32)
    return (mixed + blended).astype(jnp.bfloat16)


def solution(mesh):
    in_specs = (
        P(("req", "exp"), None),
        P(("req", "exp"), None),
        P(("req", "exp"), None),
        P("exp", "req", None),
        P(("req", "exp"), None, None),
        P(("req", "exp"), None),
        P(("req", "exp")),
        P(("req", "exp"), None),
        P(("req", "exp")),
        P(),
        P(),
        P(("req", "exp"), None),
        P(("req", "exp"), None),
        P("exp", None, None),
        P("exp", None, None),
    )
    out_specs = P(("req", "exp"), None)
    return jax.shard_map(
        per_device, mesh=mesh, in_specs=in_specs, out_specs=out_specs, check_vma=False
    )
```

```python
import math

import jax
import jax.numpy as jnp
from jax import lax
from jax.experimental import pallas as pl
from jax.experimental.pallas import tpu as pltpu
from jax.sharding import PartitionSpec as P

D = 1536
QUERY_HEADS = 24
KEY_VALUE_HEADS = 8
HEAD_WIDTH = 64
FF = 512
TOPK = 8
TREE_TOKENS = 32
GROUPS_PER_COLUMN = 2
PAGE_POSITIONS = 64
MAXP = 6


def ancestry(parent_rows):
    tree_size = parent_rows.shape[1]
    positions = jnp.arange(tree_size, dtype=jnp.int32)
    linked = (parent_rows[:, :, None] == positions[None, None, :]).astype(jnp.float32)
    reach = jnp.eye(tree_size, dtype=jnp.float32)[None] + linked
    for sweep in range((tree_size - 1).bit_length()):
        reach = jnp.minimum(
            jnp.einsum("bij,bjk->bik", reach, reach, precision=lax.Precision.HIGHEST),
            jnp.float32(1.0),
        )
    return reach > 0.5


def attention_kernel(groups_ref, pages_ref, lengths_ref, queries_ref, tree_ref, visible_ref, prompt_ref, *rest):
    page_refs = rest[:MAXP]
    out_ref = rest[MAXP]
    request = pl.program_id(0)
    key_value_width = KEY_VALUE_HEADS * HEAD_WIDTH
    heads_repeated = QUERY_HEADS // KEY_VALUE_HEADS
    rows = heads_repeated * TREE_TOKENS
    scale_factor = HEAD_WIDTH ** (-0.5)
    tree_visible = jnp.concatenate([visible_ref[0]] * heads_repeated, 0) > 0.5
    positions = lax.broadcasted_iota(jnp.int32, (rows, MAXP * PAGE_POSITIONS), 1)
    cache_visible = positions < lengths_ref[request]
    contract = (((1,), (1,)), ((), ()))

    for kv in range(KEY_VALUE_HEADS):
        key_at = kv * HEAD_WIDTH
        value_at = key_value_width + kv * HEAD_WIDTH
        query_rows = jnp.concatenate(
            [
                queries_ref[:, (kv * heads_repeated + j) * HEAD_WIDTH : (kv * heads_repeated + j + 1) * HEAD_WIDTH]
                for j in range(heads_repeated)
            ],
            0,
        )
        prompt_keys = prompt_ref[0, :, key_at : key_at + HEAD_WIDTH]
        prompt_values = prompt_ref[0, :, value_at : value_at + HEAD_WIDTH]
        cache_keys = jnp.concatenate([p[0, :, key_at : key_at + HEAD_WIDTH] for p in page_refs], 0)
        cache_values = jnp.concatenate([p[0, :, value_at : value_at + HEAD_WIDTH] for p in page_refs], 0)
        tree_keys = tree_ref[:, key_at : key_at + HEAD_WIDTH]
        tree_values = tree_ref[:, value_at : value_at + HEAD_WIDTH]
        prompt_scores = lax.dot_general(query_rows, prompt_keys, contract, preferred_element_type=jnp.float32) * scale_factor
        cache_scores = lax.dot_general(query_rows, cache_keys, contract, preferred_element_type=jnp.float32) * scale_factor
        tree_scores = lax.dot_general(query_rows, tree_keys, contract, preferred_element_type=jnp.float32) * scale_factor
        cache_scores = jnp.where(cache_visible, cache_scores, -jnp.inf)
        tree_scores = jnp.where(tree_visible, tree_scores, -jnp.inf)
        peak = jnp.maximum(
            jnp.maximum(jnp.max(prompt_scores, -1, keepdims=True), jnp.max(cache_scores, -1, keepdims=True)),
            jnp.max(tree_scores, -1, keepdims=True),
        )
        prompt_exp = jnp.exp(prompt_scores - peak)
        cache_exp = jnp.exp(cache_scores - peak)
        tree_exp = jnp.exp(tree_scores - peak)
        denom = (
            jnp.sum(prompt_exp, -1, keepdims=True)
            + jnp.sum(cache_exp, -1, keepdims=True)
            + jnp.sum(tree_exp, -1, keepdims=True)
        )
        numer = (
            jnp.dot(prompt_exp.astype(jnp.bfloat16), prompt_values, preferred_element_type=jnp.float32)
            + jnp.dot(cache_exp.astype(jnp.bfloat16), cache_values, preferred_element_type=jnp.float32)
            + jnp.dot(tree_exp.astype(jnp.bfloat16), tree_values, preferred_element_type=jnp.float32)
        )
        result = (numer / denom).astype(jnp.bfloat16)
        for j in range(heads_repeated):
            head = kv * heads_repeated + j
            out_ref[:, head * HEAD_WIDTH : (head + 1) * HEAD_WIDTH] = result[j * TREE_TOKENS : (j + 1) * TREE_TOKENS]


def attend(queries, draft_kv, piece, cache_page_store, page_table, cache_len, parents, groups):
    count_of_tokens, width = queries.shape
    count_of_requests = page_table.shape[0]
    row_width = draft_kv.shape[1]
    store_pages = cache_page_store.shape[0]
    visible = ancestry(parents).astype(jnp.float32)
    flat_pages = jnp.clip(page_table.reshape(-1), 0, store_pages - 1).astype(jnp.int32)
    prompt_groups = jnp.clip(groups, 0, piece.shape[0] - 1).astype(jnp.int32)

    def page_spec(slot):
        return pl.BlockSpec(
            (1, PAGE_POSITIONS, row_width), lambda r, g, p, c: (p[r * MAXP + slot], 0, 0)
        )

    grid_spec = pltpu.PrefetchScalarGridSpec(
        num_scalar_prefetch=3,
        grid=(count_of_requests,),
        in_specs=[
            pl.BlockSpec((TREE_TOKENS, width), lambda r, g, p, c: (r, 0)),
            pl.BlockSpec((TREE_TOKENS, row_width), lambda r, g, p, c: (r, 0)),
            pl.BlockSpec((1, TREE_TOKENS, TREE_TOKENS), lambda r, g, p, c: (r, 0, 0)),
            pl.BlockSpec((1, piece.shape[1], row_width), lambda r, g, p, c: (g[r], 0, 0)),
        ]
        + [page_spec(slot) for slot in range(MAXP)],
        out_specs=pl.BlockSpec((TREE_TOKENS, width), lambda r, g, p, c: (r, 0)),
    )
    return pl.pallas_call(
        attention_kernel,
        grid_spec=grid_spec,
        out_shape=jax.ShapeDtypeStruct((count_of_tokens, width), jnp.bfloat16),
    )(prompt_groups, flat_pages, cache_len.astype(jnp.int32), queries, draft_kv, visible, piece, *([cache_page_store] * MAXP))


def per_device(
    resid,
    queries,
    draft_kv,
    prompt_key_value,
    cache_page_store,
    page_table,
    cache_len,
    parents,
    groups,
    w_out,
    norm_gain,
    routes,
    route_weight,
    w_in,
    w_down,
):
    local_experts = w_in.shape[0]
    exp_devices = lax.axis_size("exp")
    experts_all = local_experts * exp_devices
    count_of_tokens = routes.shape[0]
    every_expert = jnp.arange(experts_all, dtype=jnp.int32)
    gate_local = jnp.sum(
        jnp.where(routes[:, :, None] == every_expert[None, None, :], route_weight[:, :, None], jnp.float32(0.0)),
        1,
    )
    gate_gathered = lax.all_gather(gate_local, "exp", axis=0, tiled=True)
    gate = lax.dynamic_slice_in_dim(gate_gathered, lax.axis_index("exp") * local_experts, local_experts, 1)
    gate = gate.reshape(exp_devices, count_of_tokens, local_experts)
    piece = lax.all_gather(prompt_key_value, "req", axis=1, tiled=True)
    gate, piece = lax.optimization_barrier((gate, piece))
    attended = attend(queries, draft_kv, piece, cache_page_store, page_table, cache_len, parents, groups)
    mixed = resid.astype(jnp.float32) + jnp.dot(attended, w_out, preferred_element_type=jnp.float32)
    spread = jnp.mean(mixed * mixed, -1, keepdims=True)
    normed = (mixed * lax.rsqrt(spread + 1e-05) * norm_gain).astype(jnp.bfloat16)
    chunks = 1
    span = count_of_tokens // chunks
    pieces = []
    for chunk in range(chunks):
        rows = normed[chunk * span : (chunk + 1) * span]
        gathered = lax.all_gather(rows, "exp", axis=0, tiled=True)
        chunk_gate = gate[:, chunk * span : (chunk + 1) * span].reshape(exp_devices * span, local_experts)
        both = jnp.einsum("td,edf->etf", gathered, w_in, preferred_element_type=jnp.float32)
        act = (jax.nn.silu(both[..., :FF]) * both[..., FF:]).astype(jnp.bfloat16)
        result = jnp.einsum("etf,efd->etd", act, w_down, preferred_element_type=jnp.float32).astype(
            jnp.bfloat16
        )
        partial = jnp.sum(jnp.transpose(chunk_gate)[..., None] * result.astype(jnp.float32), 0)
        pieces.append(
            lax.psum_scatter(partial.astype(jnp.bfloat16), "exp", scatter_dimension=0, tiled=True)
        )
    blended = jnp.concatenate(pieces, 0).astype(jnp.float32)
    return (mixed + blended).astype(jnp.bfloat16)


def solution(mesh):
    in_specs = (
        P(("req", "exp"), None),
        P(("req", "exp"), None),
        P(("req", "exp"), None),
        P("exp", "req", None),
        P(("req", "exp"), None, None),
        P(("req", "exp"), None),
        P(("req", "exp")),
        P(("req", "exp"), None),
        P(("req", "exp")),
        P(),
        P(),
        P(("req", "exp"), None),
        P(("req", "exp"), None),
        P("exp", None, None),
        P("exp", None, None),
    )
    out_specs = P(("req", "exp"), None)
    return jax.shard_map(
        per_device, mesh=mesh, in_specs=in_specs, out_specs=out_specs, check_vma=False
    )
```

```python
import math

import jax
import jax.numpy as jnp
from jax import lax
from jax.experimental import pallas as pl
from jax.experimental.pallas import tpu as pltpu
from jax.sharding import PartitionSpec as P

D = 1536
QUERY_HEADS = 24
KEY_VALUE_HEADS = 8
HEAD_WIDTH = 64
FF = 512
TOPK = 8
TREE_TOKENS = 32
GROUPS_PER_COLUMN = 2
PAGE_POSITIONS = 64
MAXP = 6


def ancestry(parent_rows):
    tree_size = parent_rows.shape[1]
    positions = jnp.arange(tree_size, dtype=jnp.int32)
    linked = (parent_rows[:, :, None] == positions[None, None, :]).astype(jnp.float32)
    reach = jnp.eye(tree_size, dtype=jnp.float32)[None] + linked
    for sweep in range((tree_size - 1).bit_length()):
        reach = jnp.minimum(
            jnp.einsum("bij,bjk->bik", reach, reach, precision=lax.Precision.HIGHEST),
            jnp.float32(1.0),
        )
    return reach > 0.5


def attention_kernel(groups_ref, pages_ref, lengths_ref, queries_ref, tree_ref, visible_ref, prompt_ref, *rest):
    page_refs = rest[:MAXP]
    out_ref = rest[MAXP]
    request = pl.program_id(0)
    key_value_width = KEY_VALUE_HEADS * HEAD_WIDTH
    heads_repeated = QUERY_HEADS // KEY_VALUE_HEADS
    rows = heads_repeated * TREE_TOKENS
    scale_factor = HEAD_WIDTH ** (-0.5)
    tree_visible = jnp.concatenate([visible_ref[0]] * heads_repeated, 0) > 0.5
    positions = lax.broadcasted_iota(jnp.int32, (rows, MAXP * PAGE_POSITIONS), 1)
    cache_visible = positions < lengths_ref[request]
    contract = (((1,), (1,)), ((), ()))

    for kv in range(KEY_VALUE_HEADS):
        key_at = kv * HEAD_WIDTH
        value_at = key_value_width + kv * HEAD_WIDTH
        query_rows = jnp.concatenate(
            [
                queries_ref[:, (kv * heads_repeated + j) * HEAD_WIDTH : (kv * heads_repeated + j + 1) * HEAD_WIDTH]
                for j in range(heads_repeated)
            ],
            0,
        )
        prompt_keys = prompt_ref[0, :, key_at : key_at + HEAD_WIDTH]
        prompt_values = prompt_ref[0, :, value_at : value_at + HEAD_WIDTH]
        cache_keys = jnp.concatenate([p[0, :, key_at : key_at + HEAD_WIDTH] for p in page_refs], 0)
        cache_values = jnp.concatenate([p[0, :, value_at : value_at + HEAD_WIDTH] for p in page_refs], 0)
        tree_keys = tree_ref[:, key_at : key_at + HEAD_WIDTH]
        tree_values = tree_ref[:, value_at : value_at + HEAD_WIDTH]
        prompt_scores = lax.dot_general(query_rows, prompt_keys, contract, preferred_element_type=jnp.float32) * scale_factor
        cache_scores = lax.dot_general(query_rows, cache_keys, contract, preferred_element_type=jnp.float32) * scale_factor
        tree_scores = lax.dot_general(query_rows, tree_keys, contract, preferred_element_type=jnp.float32) * scale_factor
        cache_scores = jnp.where(cache_visible, cache_scores, -jnp.inf)
        tree_scores = jnp.where(tree_visible, tree_scores, -jnp.inf)
        peak = jnp.maximum(
            jnp.maximum(jnp.max(prompt_scores, -1, keepdims=True), jnp.max(cache_scores, -1, keepdims=True)),
            jnp.max(tree_scores, -1, keepdims=True),
        )
        prompt_exp = jnp.exp(prompt_scores - peak)
        cache_exp = jnp.exp(cache_scores - peak)
        tree_exp = jnp.exp(tree_scores - peak)
        denom = (
            jnp.sum(prompt_exp, -1, keepdims=True)
            + jnp.sum(cache_exp, -1, keepdims=True)
            + jnp.sum(tree_exp, -1, keepdims=True)
        )
        numer = (
            jnp.dot(prompt_exp.astype(jnp.bfloat16), prompt_values, preferred_element_type=jnp.float32)
            + jnp.dot(cache_exp.astype(jnp.bfloat16), cache_values, preferred_element_type=jnp.float32)
            + jnp.dot(tree_exp.astype(jnp.bfloat16), tree_values, preferred_element_type=jnp.float32)
        )
        result = (numer / denom).astype(jnp.bfloat16)
        for j in range(heads_repeated):
            head = kv * heads_repeated + j
            out_ref[:, head * HEAD_WIDTH : (head + 1) * HEAD_WIDTH] = result[j * TREE_TOKENS : (j + 1) * TREE_TOKENS]


def attend(queries, draft_kv, piece, cache_page_store, page_table, cache_len, parents, groups):
    count_of_tokens, width = queries.shape
    count_of_requests = page_table.shape[0]
    row_width = draft_kv.shape[1]
    store_pages = cache_page_store.shape[0]
    visible = ancestry(parents).astype(jnp.float32)
    flat_pages = jnp.clip(page_table.reshape(-1), 0, store_pages - 1).astype(jnp.int32)
    prompt_groups = jnp.clip(groups, 0, piece.shape[0] - 1).astype(jnp.int32)

    def page_spec(slot):
        return pl.BlockSpec(
            (1, PAGE_POSITIONS, row_width), lambda r, g, p, c: (p[r * MAXP + slot], 0, 0)
        )

    grid_spec = pltpu.PrefetchScalarGridSpec(
        num_scalar_prefetch=3,
        grid=(count_of_requests,),
        in_specs=[
            pl.BlockSpec((TREE_TOKENS, width), lambda r, g, p, c: (r, 0)),
            pl.BlockSpec((TREE_TOKENS, row_width), lambda r, g, p, c: (r, 0)),
            pl.BlockSpec((1, TREE_TOKENS, TREE_TOKENS), lambda r, g, p, c: (r, 0, 0)),
            pl.BlockSpec((1, piece.shape[1], row_width), lambda r, g, p, c: (g[r], 0, 0)),
        ]
        + [page_spec(slot) for slot in range(MAXP)],
        out_specs=pl.BlockSpec((TREE_TOKENS, width), lambda r, g, p, c: (r, 0)),
    )
    return pl.pallas_call(
        attention_kernel,
        grid_spec=grid_spec,
        out_shape=jax.ShapeDtypeStruct((count_of_tokens, width), jnp.bfloat16),
    )(prompt_groups, flat_pages, cache_len.astype(jnp.int32), queries, draft_kv, visible, piece, *([cache_page_store] * MAXP))


def run_experts(rows, row_gate, w_in, w_down):
    both = jnp.einsum("td,edf->etf", rows, w_in, preferred_element_type=jnp.float32)
    act = (jax.nn.silu(both[..., :FF]) * both[..., FF:]).astype(jnp.bfloat16)
    result = jnp.einsum("etf,efd->etd", act, w_down, preferred_element_type=jnp.float32).astype(jnp.bfloat16)
    return jnp.sum(jnp.transpose(row_gate)[..., None] * result.astype(jnp.float32), 0)


def exchange_experts(normed, gate, w_in, w_down):
    devices = lax.axis_size("exp")
    count_of_tokens, width = normed.shape
    if devices % 2 != 0:
        rows = lax.all_gather(normed, "exp", axis=0, tiled=True)
        partial = run_experts(rows, gate, w_in, w_down)
        return lax.psum_scatter(partial.astype(jnp.bfloat16), "exp", scatter_dimension=0, tiled=True).astype(jnp.float32)
    half = devices // 2
    me = lax.axis_index("exp")
    core = me % 2
    chip = me // 2

    def chip_shift(x, shift):
        pairs = [(2 * c + b, 2 * ((c + shift) % half) + b) for c in range(half) for b in range(2)]
        return lax.ppermute(x, "exp", pairs)

    def sibling(x):
        return lax.ppermute(x, "exp", [(i, i ^ 1) for i in range(devices)])

    same_core = jnp.stack([normed] + [chip_shift(normed, d) for d in range(1, half)], 0)
    other_core = sibling(same_core)
    rows = jnp.concatenate([same_core, other_core], 0).reshape(devices * count_of_tokens, width)
    chip_of = (chip - jnp.arange(half, dtype=jnp.int32)) % half
    device_of = jnp.concatenate([2 * chip_of + core, 2 * chip_of + (1 - core)])
    row_gate = jnp.take(gate.reshape(devices, count_of_tokens, -1), device_of, axis=0).reshape(
        devices * count_of_tokens, -1
    )
    partial = run_experts(rows, row_gate, w_in, w_down).reshape(2, half, count_of_tokens, width)
    merged = partial[0] + sibling(partial[1].astype(jnp.bfloat16)).astype(jnp.float32)
    total = merged[0]
    for d in range(1, half):
        total = total + chip_shift(merged[d].astype(jnp.bfloat16), -d).astype(jnp.float32)
    return total


def per_device(
    resid,
    queries,
    draft_kv,
    prompt_key_value,
    cache_page_store,
    page_table,
    cache_len,
    parents,
    groups,
    w_out,
    norm_gain,
    routes,
    route_weight,
    w_in,
    w_down,
):
    local_experts = w_in.shape[0]
    exp_devices = lax.axis_size("exp")
    experts_all = local_experts * exp_devices
    count_of_tokens = routes.shape[0]
    every_expert = jnp.arange(experts_all, dtype=jnp.int32)
    gate_local = jnp.sum(
        jnp.where(routes[:, :, None] == every_expert[None, None, :], route_weight[:, :, None], jnp.float32(0.0)),
        1,
    )
    gate_gathered = lax.all_gather(gate_local, "exp", axis=0, tiled=True)
    gate = lax.dynamic_slice_in_dim(gate_gathered, lax.axis_index("exp") * local_experts, local_experts, 1)
    piece = lax.all_gather(prompt_key_value, "req", axis=1, tiled=True)
    gate, piece = lax.optimization_barrier((gate, piece))
    attended = attend(queries, draft_kv, piece, cache_page_store, page_table, cache_len, parents, groups)
    mixed = resid.astype(jnp.float32) + jnp.dot(attended, w_out, preferred_element_type=jnp.float32)
    spread = jnp.mean(mixed * mixed, -1, keepdims=True)
    normed = (mixed * lax.rsqrt(spread + 1e-05) * norm_gain).astype(jnp.bfloat16)
    blended = exchange_experts(normed, gate, w_in, w_down)
    return (mixed + blended).astype(jnp.bfloat16)


def solution(mesh):
    in_specs = (
        P(("req", "exp"), None),
        P(("req", "exp"), None),
        P(("req", "exp"), None),
        P("exp", "req", None),
        P(("req", "exp"), None, None),
        P(("req", "exp"), None),
        P(("req", "exp")),
        P(("req", "exp"), None),
        P(("req", "exp")),
        P(),
        P(),
        P(("req", "exp"), None),
        P(("req", "exp"), None),
        P("exp", None, None),
        P("exp", None, None),
    )
    out_specs = P(("req", "exp"), None)
    return jax.shard_map(
        per_device, mesh=mesh, in_specs=in_specs, out_specs=out_specs, check_vma=False
    )
```

```python
import math

import jax
import jax.numpy as jnp
from jax import lax
from jax.experimental import pallas as pl
from jax.experimental.pallas import tpu as pltpu
from jax.sharding import PartitionSpec as P

D = 1536
QUERY_HEADS = 24
KEY_VALUE_HEADS = 8
HEAD_WIDTH = 64
FF = 512
TOPK = 8
TREE_TOKENS = 32
GROUPS_PER_COLUMN = 2
PAGE_POSITIONS = 64
MAXP = 6


def ancestry(parent_rows):
    tree_size = parent_rows.shape[1]
    positions = jnp.arange(tree_size, dtype=jnp.int32)
    linked = (parent_rows[:, :, None] == positions[None, None, :]).astype(jnp.float32)
    reach = jnp.eye(tree_size, dtype=jnp.float32)[None] + linked
    for sweep in range((tree_size - 1).bit_length()):
        reach = jnp.minimum(
            jnp.einsum("bij,bjk->bik", reach, reach, precision=lax.Precision.HIGHEST),
            jnp.float32(1.0),
        )
    return reach > 0.5


def attention_kernel(groups_ref, pages_ref, lengths_ref, queries_ref, tree_ref, visible_ref, prompt_ref, *rest):
    page_refs = rest[:MAXP]
    out_ref = rest[MAXP]
    request = pl.program_id(0)
    key_value_width = KEY_VALUE_HEADS * HEAD_WIDTH
    heads_repeated = QUERY_HEADS // KEY_VALUE_HEADS
    rows = heads_repeated * TREE_TOKENS
    scale_factor = HEAD_WIDTH ** (-0.5)
    tree_visible = jnp.concatenate([visible_ref[0]] * heads_repeated, 0) > 0.5
    positions = lax.broadcasted_iota(jnp.int32, (rows, MAXP * PAGE_POSITIONS), 1)
    cache_visible = positions < lengths_ref[request]
    contract = (((1,), (1,)), ((), ()))

    for kv in range(KEY_VALUE_HEADS):
        key_at = kv * HEAD_WIDTH
        value_at = key_value_width + kv * HEAD_WIDTH
        query_rows = jnp.concatenate(
            [
                queries_ref[:, (kv * heads_repeated + j) * HEAD_WIDTH : (kv * heads_repeated + j + 1) * HEAD_WIDTH]
                for j in range(heads_repeated)
            ],
            0,
        )
        prompt_keys = prompt_ref[0, :, key_at : key_at + HEAD_WIDTH]
        prompt_values = prompt_ref[0, :, value_at : value_at + HEAD_WIDTH]
        cache_keys = jnp.concatenate([p[0, :, key_at : key_at + HEAD_WIDTH] for p in page_refs], 0)
        cache_values = jnp.concatenate([p[0, :, value_at : value_at + HEAD_WIDTH] for p in page_refs], 0)
        tree_keys = tree_ref[:, key_at : key_at + HEAD_WIDTH]
        tree_values = tree_ref[:, value_at : value_at + HEAD_WIDTH]
        prompt_scores = lax.dot_general(query_rows, prompt_keys, contract, preferred_element_type=jnp.float32) * scale_factor
        cache_scores = lax.dot_general(query_rows, cache_keys, contract, preferred_element_type=jnp.float32) * scale_factor
        tree_scores = lax.dot_general(query_rows, tree_keys, contract, preferred_element_type=jnp.float32) * scale_factor
        cache_scores = jnp.where(cache_visible, cache_scores, -jnp.inf)
        tree_scores = jnp.where(tree_visible, tree_scores, -jnp.inf)
        peak = jnp.maximum(
            jnp.maximum(jnp.max(prompt_scores, -1, keepdims=True), jnp.max(cache_scores, -1, keepdims=True)),
            jnp.max(tree_scores, -1, keepdims=True),
        )
        prompt_exp = jnp.exp(prompt_scores - peak)
        cache_exp = jnp.exp(cache_scores - peak)
        tree_exp = jnp.exp(tree_scores - peak)
        denom = (
            jnp.sum(prompt_exp, -1, keepdims=True)
            + jnp.sum(cache_exp, -1, keepdims=True)
            + jnp.sum(tree_exp, -1, keepdims=True)
        )
        numer = (
            jnp.dot(prompt_exp.astype(jnp.bfloat16), prompt_values, preferred_element_type=jnp.float32)
            + jnp.dot(cache_exp.astype(jnp.bfloat16), cache_values, preferred_element_type=jnp.float32)
            + jnp.dot(tree_exp.astype(jnp.bfloat16), tree_values, preferred_element_type=jnp.float32)
        )
        result = (numer / denom).astype(jnp.bfloat16)
        for j in range(heads_repeated):
            head = kv * heads_repeated + j
            out_ref[:, head * HEAD_WIDTH : (head + 1) * HEAD_WIDTH] = result[j * TREE_TOKENS : (j + 1) * TREE_TOKENS]


def attend(queries, draft_kv, piece, cache_page_store, page_table, cache_len, parents, groups):
    count_of_tokens, width = queries.shape
    count_of_requests = page_table.shape[0]
    row_width = draft_kv.shape[1]
    store_pages = cache_page_store.shape[0]
    visible = ancestry(parents).astype(jnp.float32)
    flat_pages = jnp.clip(page_table.reshape(-1), 0, store_pages - 1).astype(jnp.int32)
    prompt_groups = jnp.clip(groups, 0, piece.shape[0] - 1).astype(jnp.int32)

    def page_spec(slot):
        return pl.BlockSpec(
            (1, PAGE_POSITIONS, row_width), lambda r, g, p, c: (p[r * MAXP + slot], 0, 0)
        )

    grid_spec = pltpu.PrefetchScalarGridSpec(
        num_scalar_prefetch=3,
        grid=(count_of_requests,),
        in_specs=[
            pl.BlockSpec((TREE_TOKENS, width), lambda r, g, p, c: (r, 0)),
            pl.BlockSpec((TREE_TOKENS, row_width), lambda r, g, p, c: (r, 0)),
            pl.BlockSpec((1, TREE_TOKENS, TREE_TOKENS), lambda r, g, p, c: (r, 0, 0)),
            pl.BlockSpec((1, piece.shape[1], row_width), lambda r, g, p, c: (g[r], 0, 0)),
        ]
        + [page_spec(slot) for slot in range(MAXP)],
        out_specs=pl.BlockSpec((TREE_TOKENS, width), lambda r, g, p, c: (r, 0)),
    )
    return pl.pallas_call(
        attention_kernel,
        grid_spec=grid_spec,
        out_shape=jax.ShapeDtypeStruct((count_of_tokens, width), jnp.bfloat16),
    )(prompt_groups, flat_pages, cache_len.astype(jnp.int32), queries, draft_kv, visible, piece, *([cache_page_store] * MAXP))


def run_experts(rows, row_gate, w_in, w_down):
    both = jnp.einsum("td,edf->etf", rows, w_in, preferred_element_type=jnp.float32)
    act = (jax.nn.silu(both[..., :FF]) * both[..., FF:]).astype(jnp.bfloat16)
    result = jnp.einsum("etf,efd->etd", act, w_down, preferred_element_type=jnp.float32).astype(jnp.bfloat16)
    return jnp.sum(jnp.transpose(row_gate)[..., None] * result.astype(jnp.float32), 0)


def exchange_experts(normed, gate, w_in, w_down):
    devices = lax.axis_size("exp")
    count_of_tokens, width = normed.shape
    if devices % 2 != 0:
        rows = lax.all_gather(normed, "exp", axis=0, tiled=True)
        partial = run_experts(rows, gate, w_in, w_down)
        return lax.psum_scatter(partial.astype(jnp.bfloat16), "exp", scatter_dimension=0, tiled=True).astype(jnp.float32)
    half = devices // 2
    me = lax.axis_index("exp")
    core = me % 2
    chip = me // 2

    def chip_shift(x, shift):
        pairs = [(2 * c + b, 2 * ((c + shift) % half) + b) for c in range(half) for b in range(2)]
        return lax.ppermute(x, "exp", pairs)

    def sibling(x):
        return lax.ppermute(x, "exp", [(i, i ^ 1) for i in range(devices)])

    gate_blocks = gate.reshape(devices, count_of_tokens, -1)

    def block_gate(device):
        return lax.dynamic_index_in_dim(gate_blocks, device, 0, keepdims=False)

    same_core = [normed] + [chip_shift(normed, d) for d in range(1, half)]
    other_core = [sibling(rows) for rows in same_core]
    total = None
    for d in range(half):
        source_chip = (chip - d) % half
        other_partial = run_experts(other_core[d], block_gate(2 * source_chip + 1 - core), w_in, w_down)
        same_partial = run_experts(same_core[d], block_gate(2 * source_chip + core), w_in, w_down)
        merged = same_partial + sibling(other_partial.astype(jnp.bfloat16)).astype(jnp.float32)
        if d == 0:
            total = merged if total is None else total + merged
        else:
            arrived = chip_shift(merged.astype(jnp.bfloat16), -d).astype(jnp.float32)
            total = arrived if total is None else total + arrived
    return total


def per_device(
    resid,
    queries,
    draft_kv,
    prompt_key_value,
    cache_page_store,
    page_table,
    cache_len,
    parents,
    groups,
    w_out,
    norm_gain,
    routes,
    route_weight,
    w_in,
    w_down,
):
    local_experts = w_in.shape[0]
    exp_devices = lax.axis_size("exp")
    experts_all = local_experts * exp_devices
    count_of_tokens = routes.shape[0]
    every_expert = jnp.arange(experts_all, dtype=jnp.int32)
    gate_local = jnp.sum(
        jnp.where(routes[:, :, None] == every_expert[None, None, :], route_weight[:, :, None], jnp.float32(0.0)),
        1,
    )
    gate_gathered = lax.all_gather(gate_local, "exp", axis=0, tiled=True)
    gate = lax.dynamic_slice_in_dim(gate_gathered, lax.axis_index("exp") * local_experts, local_experts, 1)
    piece = lax.all_gather(prompt_key_value, "req", axis=1, tiled=True)
    gate, piece = lax.optimization_barrier((gate, piece))
    attended = attend(queries, draft_kv, piece, cache_page_store, page_table, cache_len, parents, groups)
    mixed = resid.astype(jnp.float32) + jnp.dot(attended, w_out, preferred_element_type=jnp.float32)
    spread = jnp.mean(mixed * mixed, -1, keepdims=True)
    normed = (mixed * lax.rsqrt(spread + 1e-05) * norm_gain).astype(jnp.bfloat16)
    blended = exchange_experts(normed, gate, w_in, w_down)
    return (mixed + blended).astype(jnp.bfloat16)


def solution(mesh):
    in_specs = (
        P(("req", "exp"), None),
        P(("req", "exp"), None),
        P(("req", "exp"), None),
        P("exp", "req", None),
        P(("req", "exp"), None, None),
        P(("req", "exp"), None),
        P(("req", "exp")),
        P(("req", "exp"), None),
        P(("req", "exp")),
        P(),
        P(),
        P(("req", "exp"), None),
        P(("req", "exp"), None),
        P("exp", None, None),
        P("exp", None, None),
    )
    out_specs = P(("req", "exp"), None)
    return jax.shard_map(
        per_device, mesh=mesh, in_specs=in_specs, out_specs=out_specs, check_vma=False
    )
```

```python
import math

import jax
import jax.numpy as jnp
from jax import lax
from jax.experimental import pallas as pl
from jax.experimental.pallas import tpu as pltpu
from jax.sharding import PartitionSpec as P

D = 1536
QUERY_HEADS = 24
KEY_VALUE_HEADS = 8
HEAD_WIDTH = 64
FF = 512
TOPK = 8
TREE_TOKENS = 32
GROUPS_PER_COLUMN = 2
PAGE_POSITIONS = 64
MAXP = 6


def ancestry(parent_rows):
    tree_size = parent_rows.shape[1]
    positions = jnp.arange(tree_size, dtype=jnp.int32)
    linked = (parent_rows[:, :, None] == positions[None, None, :]).astype(jnp.float32)
    reach = jnp.eye(tree_size, dtype=jnp.float32)[None] + linked
    for sweep in range((tree_size - 1).bit_length()):
        reach = jnp.minimum(
            jnp.einsum("bij,bjk->bik", reach, reach, precision=lax.Precision.HIGHEST),
            jnp.float32(1.0),
        )
    return reach > 0.5


def stacked_queries(queries_ref, kv):
    heads_repeated = QUERY_HEADS // KEY_VALUE_HEADS
    return jnp.concatenate(
        [
            queries_ref[:, (kv * heads_repeated + j) * HEAD_WIDTH : (kv * heads_repeated + j + 1) * HEAD_WIDTH]
            for j in range(heads_repeated)
        ],
        0,
    )


def scores_of(query_rows, keys):
    contract = (((1,), (1,)), ((), ()))
    return lax.dot_general(query_rows, keys, contract, preferred_element_type=jnp.float32) * (HEAD_WIDTH ** (-0.5))


def local_kernel(lengths_ref, pages_ref, queries_ref, tree_ref, visible_ref, *rest):
    page_refs = rest[:MAXP]
    peak_ref, denom_ref, numer_ref = rest[MAXP:]
    request = pl.program_id(0)
    key_value_width = KEY_VALUE_HEADS * HEAD_WIDTH
    heads_repeated = QUERY_HEADS // KEY_VALUE_HEADS
    rows = heads_repeated * TREE_TOKENS
    tree_visible = jnp.concatenate([visible_ref[0]] * heads_repeated, 0) > 0.5
    positions = lax.broadcasted_iota(jnp.int32, (rows, MAXP * PAGE_POSITIONS), 1)
    cache_visible = positions < lengths_ref[request]
    for kv in range(KEY_VALUE_HEADS):
        key_at = kv * HEAD_WIDTH
        value_at = key_value_width + kv * HEAD_WIDTH
        query_rows = stacked_queries(queries_ref, kv)
        cache_keys = jnp.concatenate([p[0, :, key_at : key_at + HEAD_WIDTH] for p in page_refs], 0)
        cache_values = jnp.concatenate([p[0, :, value_at : value_at + HEAD_WIDTH] for p in page_refs], 0)
        tree_keys = tree_ref[:, key_at : key_at + HEAD_WIDTH]
        tree_values = tree_ref[:, value_at : value_at + HEAD_WIDTH]
        cache_scores = jnp.where(cache_visible, scores_of(query_rows, cache_keys), -jnp.inf)
        tree_scores = jnp.where(tree_visible, scores_of(query_rows, tree_keys), -jnp.inf)
        peak = jnp.maximum(jnp.max(cache_scores, -1, keepdims=True), jnp.max(tree_scores, -1, keepdims=True))
        cache_exp = jnp.exp(cache_scores - peak)
        tree_exp = jnp.exp(tree_scores - peak)
        peak_ref[0, kv] = peak
        denom_ref[0, kv] = jnp.sum(cache_exp, -1, keepdims=True) + jnp.sum(tree_exp, -1, keepdims=True)
        numer_ref[0, kv] = jnp.dot(
            cache_exp.astype(jnp.bfloat16), cache_values, preferred_element_type=jnp.float32
        ) + jnp.dot(tree_exp.astype(jnp.bfloat16), tree_values, preferred_element_type=jnp.float32)


def prompt_kernel(groups_ref, queries_ref, prompt_ref, peak_ref, denom_ref, numer_ref, out_ref):
    key_value_width = KEY_VALUE_HEADS * HEAD_WIDTH
    heads_repeated = QUERY_HEADS // KEY_VALUE_HEADS
    for kv in range(KEY_VALUE_HEADS):
        key_at = kv * HEAD_WIDTH
        value_at = key_value_width + kv * HEAD_WIDTH
        query_rows = stacked_queries(queries_ref, kv)
        prompt_scores = scores_of(query_rows, prompt_ref[0, :, key_at : key_at + HEAD_WIDTH])
        local_peak = peak_ref[0, kv]
        peak = jnp.maximum(local_peak, jnp.max(prompt_scores, -1, keepdims=True))
        prompt_exp = jnp.exp(prompt_scores - peak)
        decay = jnp.exp(local_peak - peak)
        denom = denom_ref[0, kv] * decay + jnp.sum(prompt_exp, -1, keepdims=True)
        numer = numer_ref[0, kv] * decay + jnp.dot(
            prompt_exp.astype(jnp.bfloat16),
            prompt_ref[0, :, value_at : value_at + HEAD_WIDTH],
            preferred_element_type=jnp.float32,
        )
        result = (numer / denom).astype(jnp.bfloat16)
        for j in range(heads_repeated):
            head = kv * heads_repeated + j
            out_ref[:, head * HEAD_WIDTH : (head + 1) * HEAD_WIDTH] = result[j * TREE_TOKENS : (j + 1) * TREE_TOKENS]


def attend_local(queries, draft_kv, cache_page_store, page_table, cache_len, parents):
    count_of_tokens, width = queries.shape
    count_of_requests = page_table.shape[0]
    row_width = draft_kv.shape[1]
    store_pages = cache_page_store.shape[0]
    rows = (QUERY_HEADS // KEY_VALUE_HEADS) * TREE_TOKENS
    visible = ancestry(parents).astype(jnp.float32)
    flat_pages = jnp.clip(page_table.reshape(-1), 0, store_pages - 1).astype(jnp.int32)

    def page_spec(slot):
        return pl.BlockSpec((1, PAGE_POSITIONS, row_width), lambda r, c, p: (p[r * MAXP + slot], 0, 0))

    def stat_spec(last):
        return pl.BlockSpec((1, KEY_VALUE_HEADS, rows, last), lambda r, c, p: (r, 0, 0, 0))

    grid_spec = pltpu.PrefetchScalarGridSpec(
        num_scalar_prefetch=2,
        grid=(count_of_requests,),
        in_specs=[
            pl.BlockSpec((TREE_TOKENS, width), lambda r, c, p: (r, 0)),
            pl.BlockSpec((TREE_TOKENS, row_width), lambda r, c, p: (r, 0)),
            pl.BlockSpec((1, TREE_TOKENS, TREE_TOKENS), lambda r, c, p: (r, 0, 0)),
        ]
        + [page_spec(slot) for slot in range(MAXP)],
        out_specs=[stat_spec(1), stat_spec(1), stat_spec(HEAD_WIDTH)],
    )
    stat_shape = (count_of_requests, KEY_VALUE_HEADS, rows)
    return pl.pallas_call(
        local_kernel,
        grid_spec=grid_spec,
        out_shape=[
            jax.ShapeDtypeStruct(stat_shape + (1,), jnp.float32),
            jax.ShapeDtypeStruct(stat_shape + (1,), jnp.float32),
            jax.ShapeDtypeStruct(stat_shape + (HEAD_WIDTH,), jnp.float32),
        ],
    )(cache_len.astype(jnp.int32), flat_pages, queries, draft_kv, visible, *([cache_page_store] * MAXP))


def attend_prompt(queries, piece, groups, peak, denom, numer):
    count_of_tokens, width = queries.shape
    count_of_requests = peak.shape[0]
    rows = peak.shape[2]
    row_width = piece.shape[2]
    prompt_groups = jnp.clip(groups, 0, piece.shape[0] - 1).astype(jnp.int32)

    def stat_spec(last):
        return pl.BlockSpec((1, KEY_VALUE_HEADS, rows, last), lambda r, g: (r, 0, 0, 0))

    grid_spec = pltpu.PrefetchScalarGridSpec(
        num_scalar_prefetch=1,
        grid=(count_of_requests,),
        in_specs=[
            pl.BlockSpec((TREE_TOKENS, width), lambda r, g: (r, 0)),
            pl.BlockSpec((1, piece.shape[1], row_width), lambda r, g: (g[r], 0, 0)),
            stat_spec(1),
            stat_spec(1),
            stat_spec(HEAD_WIDTH),
        ],
        out_specs=pl.BlockSpec((TREE_TOKENS, width), lambda r, g: (r, 0)),
    )
    return pl.pallas_call(
        prompt_kernel,
        grid_spec=grid_spec,
        out_shape=jax.ShapeDtypeStruct((count_of_tokens, width), jnp.bfloat16),
    )(prompt_groups, queries, piece, peak, denom, numer)


def attend(queries, draft_kv, piece, cache_page_store, page_table, cache_len, parents, groups):
    peak, denom, numer = attend_local(queries, draft_kv, cache_page_store, page_table, cache_len, parents)
    return attend_prompt(queries, piece, groups, peak, denom, numer)


def run_experts(rows, row_gate, w_in, w_down):
    both = jnp.einsum("td,edf->etf", rows, w_in, preferred_element_type=jnp.float32)
    act = (jax.nn.silu(both[..., :FF]) * both[..., FF:]).astype(jnp.bfloat16)
    result = jnp.einsum("etf,efd->etd", act, w_down, preferred_element_type=jnp.float32).astype(jnp.bfloat16)
    return jnp.sum(jnp.transpose(row_gate)[..., None] * result.astype(jnp.float32), 0)


def exchange_experts(normed, gate, w_in, w_down):
    devices = lax.axis_size("exp")
    count_of_tokens, width = normed.shape
    if devices % 2 != 0:
        rows = lax.all_gather(normed, "exp", axis=0, tiled=True)
        partial = run_experts(rows, gate, w_in, w_down)
        return lax.psum_scatter(partial.astype(jnp.bfloat16), "exp", scatter_dimension=0, tiled=True).astype(jnp.float32)
    half = devices // 2
    me = lax.axis_index("exp")
    core = me % 2
    chip = me // 2

    def chip_shift(x, shift):
        pairs = [(2 * c + b, 2 * ((c + shift) % half) + b) for c in range(half) for b in range(2)]
        return lax.ppermute(x, "exp", pairs)

    def sibling(x):
        return lax.ppermute(x, "exp", [(i, i ^ 1) for i in range(devices)])

    gate_blocks = gate.reshape(devices, count_of_tokens, -1)

    def block_gate(device):
        return lax.dynamic_index_in_dim(gate_blocks, device, 0, keepdims=False)

    same_core = [normed] + [chip_shift(normed, d) for d in range(1, half)]
    other_core = [sibling(rows) for rows in same_core]
    total = None
    for d in range(half):
        source_chip = (chip - d) % half
        other_partial = run_experts(other_core[d], block_gate(2 * source_chip + 1 - core), w_in, w_down)
        same_partial = run_experts(same_core[d], block_gate(2 * source_chip + core), w_in, w_down)
        merged = same_partial + sibling(other_partial.astype(jnp.bfloat16)).astype(jnp.float32)
        if d == 0:
            total = merged if total is None else total + merged
        else:
            arrived = chip_shift(merged.astype(jnp.bfloat16), -d).astype(jnp.float32)
            total = arrived if total is None else total + arrived
    return total


def per_device(
    resid,
    queries,
    draft_kv,
    prompt_key_value,
    cache_page_store,
    page_table,
    cache_len,
    parents,
    groups,
    w_out,
    norm_gain,
    routes,
    route_weight,
    w_in,
    w_down,
):
    local_experts = w_in.shape[0]
    exp_devices = lax.axis_size("exp")
    experts_all = local_experts * exp_devices
    count_of_tokens = routes.shape[0]
    every_expert = jnp.arange(experts_all, dtype=jnp.int32)
    gate_local = jnp.sum(
        jnp.where(routes[:, :, None] == every_expert[None, None, :], route_weight[:, :, None], jnp.float32(0.0)),
        1,
    )
    gate_gathered = lax.all_gather(gate_local, "exp", axis=0, tiled=True)
    gate = lax.dynamic_slice_in_dim(gate_gathered, lax.axis_index("exp") * local_experts, local_experts, 1)
    piece = lax.all_gather(prompt_key_value, "req", axis=1, tiled=True)
    gate, piece = lax.optimization_barrier((gate, piece))
    attended = attend(queries, draft_kv, piece, cache_page_store, page_table, cache_len, parents, groups)
    mixed = resid.astype(jnp.float32) + jnp.dot(attended, w_out, preferred_element_type=jnp.float32)
    spread = jnp.mean(mixed * mixed, -1, keepdims=True)
    normed = (mixed * lax.rsqrt(spread + 1e-05) * norm_gain).astype(jnp.bfloat16)
    blended = exchange_experts(normed, gate, w_in, w_down)
    return (mixed + blended).astype(jnp.bfloat16)


def solution(mesh):
    in_specs = (
        P(("req", "exp"), None),
        P(("req", "exp"), None),
        P(("req", "exp"), None),
        P("exp", "req", None),
        P(("req", "exp"), None, None),
        P(("req", "exp"), None),
        P(("req", "exp")),
        P(("req", "exp"), None),
        P(("req", "exp")),
        P(),
        P(),
        P(("req", "exp"), None),
        P(("req", "exp"), None),
        P("exp", None, None),
        P("exp", None, None),
    )
    out_specs = P(("req", "exp"), None)
    return jax.shard_map(
        per_device, mesh=mesh, in_specs=in_specs, out_specs=out_specs, check_vma=False
    )
```

```python
import math

import jax
import jax.numpy as jnp
from jax import lax
from jax.experimental import pallas as pl
from jax.experimental.pallas import tpu as pltpu
from jax.sharding import PartitionSpec as P

D = 1536
QUERY_HEADS = 24
KEY_VALUE_HEADS = 8
HEAD_WIDTH = 64
FF = 512
TOPK = 8
TREE_TOKENS = 32
GROUPS_PER_COLUMN = 2
PAGE_POSITIONS = 64
MAXP = 6


def ancestry(parent_rows):
    tree_size = parent_rows.shape[1]
    positions = jnp.arange(tree_size, dtype=jnp.int32)
    linked = (parent_rows[:, :, None] == positions[None, None, :]).astype(jnp.float32)
    reach = jnp.eye(tree_size, dtype=jnp.float32)[None] + linked
    for sweep in range((tree_size - 1).bit_length()):
        reach = jnp.minimum(
            jnp.einsum("bij,bjk->bik", reach, reach, precision=lax.Precision.HIGHEST),
            jnp.float32(1.0),
        )
    return reach > 0.5


def attention_kernel(groups_ref, pages_ref, lengths_ref, queries_ref, tree_ref, visible_ref, prompt_ref, *rest):
    page_refs = rest[:MAXP]
    out_ref = rest[MAXP]
    request = pl.program_id(0)
    key_value_width = KEY_VALUE_HEADS * HEAD_WIDTH
    heads_repeated = QUERY_HEADS // KEY_VALUE_HEADS
    rows = heads_repeated * TREE_TOKENS
    scale_factor = HEAD_WIDTH ** (-0.5)
    tree_visible = jnp.concatenate([visible_ref[0]] * heads_repeated, 0) > 0.5
    positions = lax.broadcasted_iota(jnp.int32, (rows, MAXP * PAGE_POSITIONS), 1)
    cache_visible = positions < lengths_ref[request]
    contract = (((1,), (1,)), ((), ()))

    for kv in range(KEY_VALUE_HEADS):
        key_at = kv * HEAD_WIDTH
        value_at = key_value_width + kv * HEAD_WIDTH
        query_rows = queries_ref[0, kv]
        prompt_keys = prompt_ref[0, :, key_at : key_at + HEAD_WIDTH]
        prompt_values = prompt_ref[0, :, value_at : value_at + HEAD_WIDTH]
        cache_keys = jnp.concatenate([p[0, :, key_at : key_at + HEAD_WIDTH] for p in page_refs], 0)
        cache_values = jnp.concatenate([p[0, :, value_at : value_at + HEAD_WIDTH] for p in page_refs], 0)
        tree_keys = tree_ref[:, key_at : key_at + HEAD_WIDTH]
        tree_values = tree_ref[:, value_at : value_at + HEAD_WIDTH]
        prompt_scores = lax.dot_general(query_rows, prompt_keys, contract, preferred_element_type=jnp.float32) * scale_factor
        cache_scores = lax.dot_general(query_rows, cache_keys, contract, preferred_element_type=jnp.float32) * scale_factor
        tree_scores = lax.dot_general(query_rows, tree_keys, contract, preferred_element_type=jnp.float32) * scale_factor
        cache_scores = jnp.where(cache_visible, cache_scores, -jnp.inf)
        tree_scores = jnp.where(tree_visible, tree_scores, -jnp.inf)
        peak = jnp.maximum(
            jnp.maximum(jnp.max(prompt_scores, -1, keepdims=True), jnp.max(cache_scores, -1, keepdims=True)),
            jnp.max(tree_scores, -1, keepdims=True),
        )
        prompt_exp = jnp.exp(prompt_scores - peak)
        cache_exp = jnp.exp(cache_scores - peak)
        tree_exp = jnp.exp(tree_scores - peak)
        denom = (
            jnp.sum(prompt_exp, -1, keepdims=True)
            + jnp.sum(cache_exp, -1, keepdims=True)
            + jnp.sum(tree_exp, -1, keepdims=True)
        )
        numer = (
            jnp.dot(prompt_exp.astype(jnp.bfloat16), prompt_values, preferred_element_type=jnp.float32)
            + jnp.dot(cache_exp.astype(jnp.bfloat16), cache_values, preferred_element_type=jnp.float32)
            + jnp.dot(tree_exp.astype(jnp.bfloat16), tree_values, preferred_element_type=jnp.float32)
        )
        out_ref[0, kv] = (numer / denom).astype(jnp.bfloat16)


def attend(queries, draft_kv, piece, cache_page_store, page_table, cache_len, parents, groups):
    count_of_tokens, width = queries.shape
    count_of_requests = page_table.shape[0]
    row_width = draft_kv.shape[1]
    store_pages = cache_page_store.shape[0]
    visible = ancestry(parents).astype(jnp.float32)
    flat_pages = jnp.clip(page_table.reshape(-1), 0, store_pages - 1).astype(jnp.int32)
    heads_repeated = QUERY_HEADS // KEY_VALUE_HEADS
    rows = heads_repeated * TREE_TOKENS
    head_queries = queries.reshape(count_of_requests, TREE_TOKENS, KEY_VALUE_HEADS, heads_repeated, HEAD_WIDTH)
    head_queries = head_queries.transpose(0, 2, 3, 1, 4).reshape(count_of_requests, KEY_VALUE_HEADS, rows, HEAD_WIDTH)
    prompt_groups = jnp.clip(groups, 0, piece.shape[0] - 1).astype(jnp.int32)

    def page_spec(slot):
        return pl.BlockSpec(
            (1, PAGE_POSITIONS, row_width), lambda r, g, p, c: (p[r * MAXP + slot], 0, 0)
        )

    grid_spec = pltpu.PrefetchScalarGridSpec(
        num_scalar_prefetch=3,
        grid=(count_of_requests,),
        in_specs=[
            pl.BlockSpec((1, KEY_VALUE_HEADS, rows, HEAD_WIDTH), lambda r, g, p, c: (r, 0, 0, 0)),
            pl.BlockSpec((TREE_TOKENS, row_width), lambda r, g, p, c: (r, 0)),
            pl.BlockSpec((1, TREE_TOKENS, TREE_TOKENS), lambda r, g, p, c: (r, 0, 0)),
            pl.BlockSpec((1, piece.shape[1], row_width), lambda r, g, p, c: (g[r], 0, 0)),
        ]
        + [page_spec(slot) for slot in range(MAXP)],
        out_specs=pl.BlockSpec((1, KEY_VALUE_HEADS, rows, HEAD_WIDTH), lambda r, g, p, c: (r, 0, 0, 0)),
    )
    per_head = pl.pallas_call(
        attention_kernel,
        grid_spec=grid_spec,
        out_shape=jax.ShapeDtypeStruct((count_of_requests, KEY_VALUE_HEADS, rows, HEAD_WIDTH), jnp.bfloat16),
    )(prompt_groups, flat_pages, cache_len.astype(jnp.int32), head_queries, draft_kv, visible, piece, *([cache_page_store] * MAXP))
    per_head = per_head.reshape(count_of_requests, KEY_VALUE_HEADS, heads_repeated, TREE_TOKENS, HEAD_WIDTH)
    return per_head.transpose(0, 3, 1, 2, 4).reshape(count_of_tokens, width)


def run_experts(rows, row_gate, w_in, w_down):
    both = jnp.einsum("td,edf->etf", rows, w_in, preferred_element_type=jnp.float32)
    act = (jax.nn.silu(both[..., :FF]) * both[..., FF:]).astype(jnp.bfloat16)
    result = jnp.einsum("etf,efd->etd", act, w_down, preferred_element_type=jnp.float32).astype(jnp.bfloat16)
    return jnp.sum(jnp.transpose(row_gate)[..., None] * result.astype(jnp.float32), 0)


def exchange_experts(normed, gate, w_in, w_down):
    devices = lax.axis_size("exp")
    count_of_tokens, width = normed.shape
    if devices % 2 != 0:
        rows = lax.all_gather(normed, "exp", axis=0, tiled=True)
        partial = run_experts(rows, gate, w_in, w_down)
        return lax.psum_scatter(partial.astype(jnp.bfloat16), "exp", scatter_dimension=0, tiled=True).astype(jnp.float32)
    half = devices // 2
    me = lax.axis_index("exp")
    core = me % 2
    chip = me // 2

    def chip_shift(x, shift):
        pairs = [(2 * c + b, 2 * ((c + shift) % half) + b) for c in range(half) for b in range(2)]
        return lax.ppermute(x, "exp", pairs)

    def sibling(x):
        return lax.ppermute(x, "exp", [(i, i ^ 1) for i in range(devices)])

    gate_blocks = gate.reshape(devices, count_of_tokens, -1)

    def block_gate(device):
        return lax.dynamic_index_in_dim(gate_blocks, device, 0, keepdims=False)

    same_core = [normed] + [chip_shift(normed, d) for d in range(1, half)]
    other_core = [sibling(rows) for rows in same_core]
    total = None
    for d in range(half):
        source_chip = (chip - d) % half
        other_partial = run_experts(other_core[d], block_gate(2 * source_chip + 1 - core), w_in, w_down)
        same_partial = run_experts(same_core[d], block_gate(2 * source_chip + core), w_in, w_down)
        merged = same_partial + sibling(other_partial.astype(jnp.bfloat16)).astype(jnp.float32)
        if d == 0:
            total = merged if total is None else total + merged
        else:
            arrived = chip_shift(merged.astype(jnp.bfloat16), -d).astype(jnp.float32)
            total = arrived if total is None else total + arrived
    return total


def per_device(
    resid,
    queries,
    draft_kv,
    prompt_key_value,
    cache_page_store,
    page_table,
    cache_len,
    parents,
    groups,
    w_out,
    norm_gain,
    routes,
    route_weight,
    w_in,
    w_down,
):
    local_experts = w_in.shape[0]
    exp_devices = lax.axis_size("exp")
    experts_all = local_experts * exp_devices
    count_of_tokens = routes.shape[0]
    every_expert = jnp.arange(experts_all, dtype=jnp.int32)
    gate_local = jnp.sum(
        jnp.where(routes[:, :, None] == every_expert[None, None, :], route_weight[:, :, None], jnp.float32(0.0)),
        1,
    )
    gate_gathered = lax.all_gather(gate_local, "exp", axis=0, tiled=True)
    gate = lax.dynamic_slice_in_dim(gate_gathered, lax.axis_index("exp") * local_experts, local_experts, 1)
    piece = lax.all_gather(prompt_key_value, "req", axis=1, tiled=True)
    gate, piece = lax.optimization_barrier((gate, piece))
    attended = attend(queries, draft_kv, piece, cache_page_store, page_table, cache_len, parents, groups)
    mixed = resid.astype(jnp.float32) + jnp.dot(attended, w_out, preferred_element_type=jnp.float32)
    spread = jnp.mean(mixed * mixed, -1, keepdims=True)
    normed = (mixed * lax.rsqrt(spread + 1e-05) * norm_gain).astype(jnp.bfloat16)
    blended = exchange_experts(normed, gate, w_in, w_down)
    return (mixed + blended).astype(jnp.bfloat16)


def solution(mesh):
    in_specs = (
        P(("req", "exp"), None),
        P(("req", "exp"), None),
        P(("req", "exp"), None),
        P("exp", "req", None),
        P(("req", "exp"), None, None),
        P(("req", "exp"), None),
        P(("req", "exp")),
        P(("req", "exp"), None),
        P(("req", "exp")),
        P(),
        P(),
        P(("req", "exp"), None),
        P(("req", "exp"), None),
        P("exp", None, None),
        P("exp", None, None),
    )
    out_specs = P(("req", "exp"), None)
    return jax.shard_map(
        per_device, mesh=mesh, in_specs=in_specs, out_specs=out_specs, check_vma=False
    )
```

```python
import math

import jax
import jax.numpy as jnp
from jax import lax
from jax.experimental import pallas as pl
from jax.experimental.pallas import tpu as pltpu
from jax.sharding import PartitionSpec as P

D = 1536
QUERY_HEADS = 24
KEY_VALUE_HEADS = 8
HEAD_WIDTH = 64
FF = 512
TOPK = 8
TREE_TOKENS = 32
GROUPS_PER_COLUMN = 2
PAGE_POSITIONS = 64
MAXP = 6


def ancestry(parent_rows):
    tree_size = parent_rows.shape[1]
    positions = jnp.arange(tree_size, dtype=jnp.int32)
    linked = (parent_rows[:, :, None] == positions[None, None, :]).astype(jnp.float32)
    reach = jnp.eye(tree_size, dtype=jnp.float32)[None] + linked
    for sweep in range((tree_size - 1).bit_length()):
        reach = jnp.minimum(
            jnp.einsum("bij,bjk->bik", reach, reach, precision=lax.Precision.HIGHEST),
            jnp.float32(1.0),
        )
    return reach > 0.5


def attention_kernel(groups_ref, pages_ref, lengths_ref, queries_ref, tree_ref, visible_ref, prompt_ref, *rest):
    page_refs = rest[:MAXP]
    out_ref = rest[MAXP]
    request = pl.program_id(0)
    key_value_width = KEY_VALUE_HEADS * HEAD_WIDTH
    heads_repeated = QUERY_HEADS // KEY_VALUE_HEADS
    rows = heads_repeated * TREE_TOKENS
    scale_factor = HEAD_WIDTH ** (-0.5)
    tree_visible = jnp.concatenate([visible_ref[0]] * heads_repeated, 0) > 0.5
    positions = lax.broadcasted_iota(jnp.int32, (rows, MAXP * PAGE_POSITIONS), 1)
    cache_visible = positions < lengths_ref[request]
    contract = (((1,), (1,)), ((), ()))

    for kv in range(KEY_VALUE_HEADS):
        key_at = kv * HEAD_WIDTH
        value_at = key_value_width + kv * HEAD_WIDTH
        query_rows = jnp.concatenate(
            [
                queries_ref[:, (kv * heads_repeated + j) * HEAD_WIDTH : (kv * heads_repeated + j + 1) * HEAD_WIDTH]
                for j in range(heads_repeated)
            ],
            0,
        )
        prompt_keys = prompt_ref[0, :, key_at : key_at + HEAD_WIDTH]
        prompt_values = prompt_ref[0, :, value_at : value_at + HEAD_WIDTH]
        cache_keys = jnp.concatenate([p[0, :, key_at : key_at + HEAD_WIDTH] for p in page_refs], 0)
        cache_values = jnp.concatenate([p[0, :, value_at : value_at + HEAD_WIDTH] for p in page_refs], 0)
        tree_keys = tree_ref[:, key_at : key_at + HEAD_WIDTH]
        tree_values = tree_ref[:, value_at : value_at + HEAD_WIDTH]
        prompt_scores = lax.dot_general(query_rows, prompt_keys, contract, preferred_element_type=jnp.float32) * scale_factor
        cache_scores = lax.dot_general(query_rows, cache_keys, contract, preferred_element_type=jnp.float32) * scale_factor
        tree_scores = lax.dot_general(query_rows, tree_keys, contract, preferred_element_type=jnp.float32) * scale_factor
        cache_scores = jnp.where(cache_visible, cache_scores, -jnp.inf)
        tree_scores = jnp.where(tree_visible, tree_scores, -jnp.inf)
        peak = jnp.maximum(
            jnp.maximum(jnp.max(prompt_scores, -1, keepdims=True), jnp.max(cache_scores, -1, keepdims=True)),
            jnp.max(tree_scores, -1, keepdims=True),
        )
        prompt_exp = jnp.exp(prompt_scores - peak)
        cache_exp = jnp.exp(cache_scores - peak)
        tree_exp = jnp.exp(tree_scores - peak)
        denom = (
            jnp.sum(prompt_exp, -1, keepdims=True)
            + jnp.sum(cache_exp, -1, keepdims=True)
            + jnp.sum(tree_exp, -1, keepdims=True)
        )
        numer = (
            jnp.dot(prompt_exp.astype(jnp.bfloat16), prompt_values, preferred_element_type=jnp.float32)
            + jnp.dot(cache_exp.astype(jnp.bfloat16), cache_values, preferred_element_type=jnp.float32)
            + jnp.dot(tree_exp.astype(jnp.bfloat16), tree_values, preferred_element_type=jnp.float32)
        )
        result = (numer / denom).astype(jnp.bfloat16)
        for j in range(heads_repeated):
            head = kv * heads_repeated + j
            out_ref[:, head * HEAD_WIDTH : (head + 1) * HEAD_WIDTH] = result[j * TREE_TOKENS : (j + 1) * TREE_TOKENS]


def attend(queries, draft_kv, piece, cache_page_store, page_table, cache_len, parents, groups):
    count_of_tokens, width = queries.shape
    count_of_requests = page_table.shape[0]
    row_width = draft_kv.shape[1]
    store_pages = cache_page_store.shape[0]
    visible = ancestry(parents).astype(jnp.float32)
    flat_pages = jnp.clip(page_table.reshape(-1), 0, store_pages - 1).astype(jnp.int32)
    prompt_groups = jnp.clip(groups, 0, piece.shape[0] - 1).astype(jnp.int32)

    def page_spec(slot):
        return pl.BlockSpec(
            (1, PAGE_POSITIONS, row_width), lambda r, g, p, c: (p[r * MAXP + slot], 0, 0)
        )

    grid_spec = pltpu.PrefetchScalarGridSpec(
        num_scalar_prefetch=3,
        grid=(count_of_requests,),
        in_specs=[
            pl.BlockSpec((TREE_TOKENS, width), lambda r, g, p, c: (r, 0)),
            pl.BlockSpec((TREE_TOKENS, row_width), lambda r, g, p, c: (r, 0)),
            pl.BlockSpec((1, TREE_TOKENS, TREE_TOKENS), lambda r, g, p, c: (r, 0, 0)),
            pl.BlockSpec((1, piece.shape[1], row_width), lambda r, g, p, c: (g[r], 0, 0)),
        ]
        + [page_spec(slot) for slot in range(MAXP)],
        out_specs=pl.BlockSpec((TREE_TOKENS, width), lambda r, g, p, c: (r, 0)),
    )
    return pl.pallas_call(
        attention_kernel,
        grid_spec=grid_spec,
        out_shape=jax.ShapeDtypeStruct((count_of_tokens, width), jnp.bfloat16),
    )(prompt_groups, flat_pages, cache_len.astype(jnp.int32), queries, draft_kv, visible, piece, *([cache_page_store] * MAXP))


def run_experts(rows, row_gate, w_in, w_down):
    both = jnp.einsum("td,edf->etf", rows, w_in, preferred_element_type=jnp.float32)
    act = (jax.nn.silu(both[..., :FF]) * both[..., FF:]).astype(jnp.bfloat16)
    result = jnp.einsum("etf,efd->etd", act, w_down, preferred_element_type=jnp.float32).astype(jnp.bfloat16)
    return jnp.sum(jnp.transpose(row_gate)[..., None] * result.astype(jnp.float32), 0)


def exchange_experts(normed, gate, w_in, w_down):
    devices = lax.axis_size("exp")
    count_of_tokens, width = normed.shape
    if devices % 2 != 0:
        rows = lax.all_gather(normed, "exp", axis=0, tiled=True)
        partial = run_experts(rows, gate, w_in, w_down)
        return lax.psum_scatter(partial.astype(jnp.bfloat16), "exp", scatter_dimension=0, tiled=True).astype(jnp.float32)
    half = devices // 2
    me = lax.axis_index("exp")
    core = me % 2
    chip = me // 2

    def chip_shift(x, shift):
        pairs = [(2 * c + b, 2 * ((c + shift) % half) + b) for c in range(half) for b in range(2)]
        return lax.ppermute(x, "exp", pairs)

    def sibling(x):
        return lax.ppermute(x, "exp", [(i, i ^ 1) for i in range(devices)])

    gate_blocks = gate.reshape(devices, count_of_tokens, -1)

    def block_gate(device):
        return lax.dynamic_index_in_dim(gate_blocks, device, 0, keepdims=False)

    same_core = [normed] + [chip_shift(normed, d) for d in range(1, half)]
    other_core = [sibling(rows) for rows in same_core]
    total = None
    for d in range(half):
        source_chip = (chip - d) % half
        other_partial = run_experts(other_core[d], block_gate(2 * source_chip + 1 - core), w_in, w_down)
        same_partial = run_experts(same_core[d], block_gate(2 * source_chip + core), w_in, w_down)
        merged = same_partial + sibling(other_partial.astype(jnp.bfloat16)).astype(jnp.float32)
        if d == 0:
            total = merged if total is None else total + merged
        else:
            arrived = chip_shift(merged.astype(jnp.bfloat16), -d).astype(jnp.float32)
            total = arrived if total is None else total + arrived
    return total


def per_device(
    resid,
    queries,
    draft_kv,
    prompt_key_value,
    cache_page_store,
    page_table,
    cache_len,
    parents,
    groups,
    w_out,
    norm_gain,
    routes,
    route_weight,
    w_in,
    w_down,
):
    local_experts = w_in.shape[0]
    exp_devices = lax.axis_size("exp")
    experts_all = local_experts * exp_devices
    count_of_tokens = routes.shape[0]
    every_expert = jnp.arange(experts_all, dtype=jnp.int32)
    gate_local = jnp.sum(
        jnp.where(routes[:, :, None] == every_expert[None, None, :], route_weight[:, :, None], jnp.float32(0.0)),
        1,
    )
    gate_gathered = lax.all_gather(gate_local, "exp", axis=0, tiled=True)
    gate = lax.dynamic_slice_in_dim(gate_gathered, lax.axis_index("exp") * local_experts, local_experts, 1)
    columns = lax.axis_size("req")
    piece = jnp.concatenate(
        [prompt_key_value]
        + [
            lax.ppermute(prompt_key_value, "req", [(s, (s + d) % columns) for s in range(columns)])
            for d in range(1, columns)
        ],
        1,
    )
    gate, piece = lax.optimization_barrier((gate, piece))
    attended = attend(queries, draft_kv, piece, cache_page_store, page_table, cache_len, parents, groups)
    mixed = resid.astype(jnp.float32) + jnp.dot(attended, w_out, preferred_element_type=jnp.float32)
    spread = jnp.mean(mixed * mixed, -1, keepdims=True)
    normed = (mixed * lax.rsqrt(spread + 1e-05) * norm_gain).astype(jnp.bfloat16)
    blended = exchange_experts(normed, gate, w_in, w_down)
    return (mixed + blended).astype(jnp.bfloat16)


def solution(mesh):
    in_specs = (
        P(("req", "exp"), None),
        P(("req", "exp"), None),
        P(("req", "exp"), None),
        P("exp", "req", None),
        P(("req", "exp"), None, None),
        P(("req", "exp"), None),
        P(("req", "exp")),
        P(("req", "exp"), None),
        P(("req", "exp")),
        P(),
        P(),
        P(("req", "exp"), None),
        P(("req", "exp"), None),
        P("exp", None, None),
        P("exp", None, None),
    )
    out_specs = P(("req", "exp"), None)
    return jax.shard_map(
        per_device, mesh=mesh, in_specs=in_specs, out_specs=out_specs, check_vma=False
    )
```

```python
import math

import jax
import jax.numpy as jnp
from jax import lax
from jax.experimental import pallas as pl
from jax.experimental.pallas import tpu as pltpu
from jax.sharding import PartitionSpec as P

D = 1536
QUERY_HEADS = 24
KEY_VALUE_HEADS = 8
HEAD_WIDTH = 64
FF = 512
TOPK = 8
TREE_TOKENS = 32
GROUPS_PER_COLUMN = 2
PAGE_POSITIONS = 64
MAXP = 6


def ancestry(parent_rows):
    tree_size = parent_rows.shape[1]
    positions = jnp.arange(tree_size, dtype=jnp.int32)
    linked = (parent_rows[:, :, None] == positions[None, None, :]).astype(jnp.float32)
    reach = jnp.eye(tree_size, dtype=jnp.float32)[None] + linked
    for sweep in range((tree_size - 1).bit_length()):
        reach = jnp.minimum(
            jnp.einsum("bij,bjk->bik", reach, reach, precision=lax.Precision.HIGHEST),
            jnp.float32(1.0),
        )
    return reach > 0.5


def attention_kernel(groups_ref, pages_ref, lengths_ref, queries_ref, tree_ref, visible_ref, *rest):
    prompt_refs = rest[: len(rest) - MAXP - 1]
    page_refs = rest[len(prompt_refs) : len(prompt_refs) + MAXP]
    out_ref = rest[-1]
    request = pl.program_id(0)
    key_value_width = KEY_VALUE_HEADS * HEAD_WIDTH
    heads_repeated = QUERY_HEADS // KEY_VALUE_HEADS
    rows = heads_repeated * TREE_TOKENS
    scale_factor = HEAD_WIDTH ** (-0.5)
    tree_visible = jnp.concatenate([visible_ref[0]] * heads_repeated, 0) > 0.5
    positions = lax.broadcasted_iota(jnp.int32, (rows, MAXP * PAGE_POSITIONS), 1)
    cache_visible = positions < lengths_ref[request]
    contract = (((1,), (1,)), ((), ()))

    for kv in range(KEY_VALUE_HEADS):
        key_at = kv * HEAD_WIDTH
        value_at = key_value_width + kv * HEAD_WIDTH
        query_rows = jnp.concatenate(
            [
                queries_ref[:, (kv * heads_repeated + j) * HEAD_WIDTH : (kv * heads_repeated + j + 1) * HEAD_WIDTH]
                for j in range(heads_repeated)
            ],
            0,
        )
        prompt_keys = jnp.concatenate([p[0, :, key_at : key_at + HEAD_WIDTH] for p in prompt_refs], 0)
        prompt_values = jnp.concatenate([p[0, :, value_at : value_at + HEAD_WIDTH] for p in prompt_refs], 0)
        cache_keys = jnp.concatenate([p[0, :, key_at : key_at + HEAD_WIDTH] for p in page_refs], 0)
        cache_values = jnp.concatenate([p[0, :, value_at : value_at + HEAD_WIDTH] for p in page_refs], 0)
        tree_keys = tree_ref[:, key_at : key_at + HEAD_WIDTH]
        tree_values = tree_ref[:, value_at : value_at + HEAD_WIDTH]
        prompt_scores = lax.dot_general(query_rows, prompt_keys, contract, preferred_element_type=jnp.float32) * scale_factor
        cache_scores = lax.dot_general(query_rows, cache_keys, contract, preferred_element_type=jnp.float32) * scale_factor
        tree_scores = lax.dot_general(query_rows, tree_keys, contract, preferred_element_type=jnp.float32) * scale_factor
        cache_scores = jnp.where(cache_visible, cache_scores, -jnp.inf)
        tree_scores = jnp.where(tree_visible, tree_scores, -jnp.inf)
        peak = jnp.maximum(
            jnp.maximum(jnp.max(prompt_scores, -1, keepdims=True), jnp.max(cache_scores, -1, keepdims=True)),
            jnp.max(tree_scores, -1, keepdims=True),
        )
        prompt_exp = jnp.exp(prompt_scores - peak)
        cache_exp = jnp.exp(cache_scores - peak)
        tree_exp = jnp.exp(tree_scores - peak)
        denom = (
            jnp.sum(prompt_exp, -1, keepdims=True)
            + jnp.sum(cache_exp, -1, keepdims=True)
            + jnp.sum(tree_exp, -1, keepdims=True)
        )
        numer = (
            jnp.dot(prompt_exp.astype(jnp.bfloat16), prompt_values, preferred_element_type=jnp.float32)
            + jnp.dot(cache_exp.astype(jnp.bfloat16), cache_values, preferred_element_type=jnp.float32)
            + jnp.dot(tree_exp.astype(jnp.bfloat16), tree_values, preferred_element_type=jnp.float32)
        )
        result = (numer / denom).astype(jnp.bfloat16)
        for j in range(heads_repeated):
            head = kv * heads_repeated + j
            out_ref[:, head * HEAD_WIDTH : (head + 1) * HEAD_WIDTH] = result[j * TREE_TOKENS : (j + 1) * TREE_TOKENS]


def attend(queries, draft_kv, pieces, cache_page_store, page_table, cache_len, parents, groups):
    count_of_tokens, width = queries.shape
    count_of_requests = page_table.shape[0]
    row_width = draft_kv.shape[1]
    store_pages = cache_page_store.shape[0]
    visible = ancestry(parents).astype(jnp.float32)
    flat_pages = jnp.clip(page_table.reshape(-1), 0, store_pages - 1).astype(jnp.int32)
    prompt_groups = jnp.clip(groups, 0, pieces[0].shape[0] - 1).astype(jnp.int32)

    def page_spec(slot):
        return pl.BlockSpec(
            (1, PAGE_POSITIONS, row_width), lambda r, g, p, c: (p[r * MAXP + slot], 0, 0)
        )

    grid_spec = pltpu.PrefetchScalarGridSpec(
        num_scalar_prefetch=3,
        grid=(count_of_requests,),
        in_specs=[
            pl.BlockSpec((TREE_TOKENS, width), lambda r, g, p, c: (r, 0)),
            pl.BlockSpec((TREE_TOKENS, row_width), lambda r, g, p, c: (r, 0)),
            pl.BlockSpec((1, TREE_TOKENS, TREE_TOKENS), lambda r, g, p, c: (r, 0, 0)),
        ]
        + [pl.BlockSpec((1, part.shape[1], row_width), lambda r, g, p, c: (g[r], 0, 0)) for part in pieces]
        + [page_spec(slot) for slot in range(MAXP)],
        out_specs=pl.BlockSpec((TREE_TOKENS, width), lambda r, g, p, c: (r, 0)),
    )
    return pl.pallas_call(
        attention_kernel,
        grid_spec=grid_spec,
        out_shape=jax.ShapeDtypeStruct((count_of_tokens, width), jnp.bfloat16),
    )(prompt_groups, flat_pages, cache_len.astype(jnp.int32), queries, draft_kv, visible, *pieces, *([cache_page_store] * MAXP))


def run_experts(rows, row_gate, w_in, w_down):
    both = jnp.einsum("td,edf->etf", rows, w_in, preferred_element_type=jnp.float32)
    act = (jax.nn.silu(both[..., :FF]) * both[..., FF:]).astype(jnp.bfloat16)
    result = jnp.einsum("etf,efd->etd", act, w_down, preferred_element_type=jnp.float32).astype(jnp.bfloat16)
    return jnp.sum(jnp.transpose(row_gate)[..., None] * result.astype(jnp.float32), 0)


def exchange_experts(normed, gate, w_in, w_down):
    devices = lax.axis_size("exp")
    count_of_tokens, width = normed.shape
    if devices % 2 != 0:
        rows = lax.all_gather(normed, "exp", axis=0, tiled=True)
        partial = run_experts(rows, gate, w_in, w_down)
        return lax.psum_scatter(partial.astype(jnp.bfloat16), "exp", scatter_dimension=0, tiled=True).astype(jnp.float32)
    half = devices // 2
    me = lax.axis_index("exp")
    core = me % 2
    chip = me // 2

    def chip_shift(x, shift):
        pairs = [(2 * c + b, 2 * ((c + shift) % half) + b) for c in range(half) for b in range(2)]
        return lax.ppermute(x, "exp", pairs)

    def sibling(x):
        return lax.ppermute(x, "exp", [(i, i ^ 1) for i in range(devices)])

    gate_blocks = gate.reshape(devices, count_of_tokens, -1)

    def block_gate(device):
        return lax.dynamic_index_in_dim(gate_blocks, device, 0, keepdims=False)

    same_core = [normed] + [chip_shift(normed, d) for d in range(1, half)]
    other_core = [sibling(rows) for rows in same_core]
    total = None
    for d in range(half):
        source_chip = (chip - d) % half
        other_partial = run_experts(other_core[d], block_gate(2 * source_chip + 1 - core), w_in, w_down)
        same_partial = run_experts(same_core[d], block_gate(2 * source_chip + core), w_in, w_down)
        merged = same_partial + sibling(other_partial.astype(jnp.bfloat16)).astype(jnp.float32)
        if d == 0:
            total = merged if total is None else total + merged
        else:
            arrived = chip_shift(merged.astype(jnp.bfloat16), -d).astype(jnp.float32)
            total = arrived if total is None else total + arrived
    return total


def per_device(
    resid,
    queries,
    draft_kv,
    prompt_key_value,
    cache_page_store,
    page_table,
    cache_len,
    parents,
    groups,
    w_out,
    norm_gain,
    routes,
    route_weight,
    w_in,
    w_down,
):
    local_experts = w_in.shape[0]
    exp_devices = lax.axis_size("exp")
    experts_all = local_experts * exp_devices
    count_of_tokens = routes.shape[0]
    every_expert = jnp.arange(experts_all, dtype=jnp.int32)
    gate_local = jnp.sum(
        jnp.where(routes[:, :, None] == every_expert[None, None, :], route_weight[:, :, None], jnp.float32(0.0)),
        1,
    )
    gate_gathered = lax.all_gather(gate_local, "exp", axis=0, tiled=True)
    gate = lax.dynamic_slice_in_dim(gate_gathered, lax.axis_index("exp") * local_experts, local_experts, 1)
    columns = lax.axis_size("req")
    pieces = [prompt_key_value] + [
        lax.ppermute(prompt_key_value, "req", [(s, (s + d) % columns) for s in range(columns)])
        for d in range(1, columns)
    ]
    gate, pieces = lax.optimization_barrier((gate, pieces))
    attended = attend(queries, draft_kv, pieces, cache_page_store, page_table, cache_len, parents, groups)
    mixed = resid.astype(jnp.float32) + jnp.dot(attended, w_out, preferred_element_type=jnp.float32)
    spread = jnp.mean(mixed * mixed, -1, keepdims=True)
    normed = (mixed * lax.rsqrt(spread + 1e-05) * norm_gain).astype(jnp.bfloat16)
    blended = exchange_experts(normed, gate, w_in, w_down)
    return (mixed + blended).astype(jnp.bfloat16)


def solution(mesh):
    in_specs = (
        P(("req", "exp"), None),
        P(("req", "exp"), None),
        P(("req", "exp"), None),
        P("exp", "req", None),
        P(("req", "exp"), None, None),
        P(("req", "exp"), None),
        P(("req", "exp")),
        P(("req", "exp"), None),
        P(("req", "exp")),
        P(),
        P(),
        P(("req", "exp"), None),
        P(("req", "exp"), None),
        P("exp", None, None),
        P("exp", None, None),
    )
    out_specs = P(("req", "exp"), None)
    return jax.shard_map(
        per_device, mesh=mesh, in_specs=in_specs, out_specs=out_specs, check_vma=False
    )
```

```python
import math

import jax
import jax.numpy as jnp
from jax import lax
from jax.experimental import pallas as pl
from jax.experimental.pallas import tpu as pltpu
from jax.sharding import PartitionSpec as P

D = 1536
QUERY_HEADS = 24
KEY_VALUE_HEADS = 8
HEAD_WIDTH = 64
FF = 512
TOPK = 8
TREE_TOKENS = 32
GROUPS_PER_COLUMN = 2
PAGE_POSITIONS = 64
MAXP = 6


def ancestry(parent_rows):
    tree_size = parent_rows.shape[1]
    positions = jnp.arange(tree_size, dtype=jnp.int32)
    linked = (parent_rows[:, :, None] == positions[None, None, :]).astype(jnp.float32)
    reach = jnp.eye(tree_size, dtype=jnp.float32)[None] + linked
    for sweep in range((tree_size - 1).bit_length()):
        reach = jnp.minimum(
            jnp.einsum("bij,bjk->bik", reach, reach, precision=lax.Precision.HIGHEST),
            jnp.float32(1.0),
        )
    return reach > 0.5


def attention_kernel(groups_ref, pages_ref, lengths_ref, queries_ref, tree_ref, visible_ref, *rest):
    prompt_refs = rest[: len(rest) - MAXP - 1]
    page_refs = rest[len(prompt_refs) : len(prompt_refs) + MAXP]
    out_ref = rest[-1]
    request = pl.program_id(0)
    key_value_width = KEY_VALUE_HEADS * HEAD_WIDTH
    heads_repeated = QUERY_HEADS // KEY_VALUE_HEADS
    rows = heads_repeated * TREE_TOKENS
    scale_factor = HEAD_WIDTH ** (-0.5)
    tree_visible = jnp.concatenate([visible_ref[0]] * heads_repeated, 0) > 0.5
    positions = lax.broadcasted_iota(jnp.int32, (rows, MAXP * PAGE_POSITIONS), 1)
    cache_visible = positions < lengths_ref[request]
    contract = (((1,), (1,)), ((), ()))

    for kv in range(KEY_VALUE_HEADS):
        key_at = kv * HEAD_WIDTH
        value_at = key_value_width + kv * HEAD_WIDTH
        query_rows = jnp.concatenate(
            [
                queries_ref[:, (kv * heads_repeated + j) * HEAD_WIDTH : (kv * heads_repeated + j + 1) * HEAD_WIDTH]
                for j in range(heads_repeated)
            ],
            0,
        )
        prompt_keys = jnp.concatenate([p[0, :, key_at : key_at + HEAD_WIDTH] for p in prompt_refs], 0)
        prompt_values = jnp.concatenate([p[0, :, value_at : value_at + HEAD_WIDTH] for p in prompt_refs], 0)
        cache_keys = jnp.concatenate([p[0, :, key_at : key_at + HEAD_WIDTH] for p in page_refs], 0)
        cache_values = jnp.concatenate([p[0, :, value_at : value_at + HEAD_WIDTH] for p in page_refs], 0)
        tree_keys = tree_ref[:, key_at : key_at + HEAD_WIDTH]
        tree_values = tree_ref[:, value_at : value_at + HEAD_WIDTH]
        prompt_scores = lax.dot_general(query_rows, prompt_keys, contract, preferred_element_type=jnp.float32) * scale_factor
        cache_scores = lax.dot_general(query_rows, cache_keys, contract, preferred_element_type=jnp.float32) * scale_factor
        tree_scores = lax.dot_general(query_rows, tree_keys, contract, preferred_element_type=jnp.float32) * scale_factor
        cache_scores = jnp.where(cache_visible, cache_scores, -jnp.inf)
        tree_scores = jnp.where(tree_visible, tree_scores, -jnp.inf)
        peak = jnp.maximum(
            jnp.maximum(jnp.max(prompt_scores, -1, keepdims=True), jnp.max(cache_scores, -1, keepdims=True)),
            jnp.max(tree_scores, -1, keepdims=True),
        )
        prompt_exp = jnp.exp(prompt_scores - peak)
        cache_exp = jnp.exp(cache_scores - peak)
        tree_exp = jnp.exp(tree_scores - peak)
        denom = (
            jnp.sum(prompt_exp, -1, keepdims=True)
            + jnp.sum(cache_exp, -1, keepdims=True)
            + jnp.sum(tree_exp, -1, keepdims=True)
        )
        numer = (
            jnp.dot(prompt_exp.astype(jnp.bfloat16), prompt_values, preferred_element_type=jnp.float32)
            + jnp.dot(cache_exp.astype(jnp.bfloat16), cache_values, preferred_element_type=jnp.float32)
            + jnp.dot(tree_exp.astype(jnp.bfloat16), tree_values, preferred_element_type=jnp.float32)
        )
        result = (numer / denom).astype(jnp.bfloat16)
        for j in range(heads_repeated):
            head = kv * heads_repeated + j
            out_ref[:, head * HEAD_WIDTH : (head + 1) * HEAD_WIDTH] = result[j * TREE_TOKENS : (j + 1) * TREE_TOKENS]


def attend(queries, draft_kv, pieces, cache_page_store, page_table, cache_len, parents, groups):
    count_of_tokens, width = queries.shape
    count_of_requests = page_table.shape[0]
    row_width = draft_kv.shape[1]
    store_pages = cache_page_store.shape[0]
    visible = ancestry(parents).astype(jnp.float32)
    flat_pages = jnp.clip(page_table.reshape(-1), 0, store_pages - 1).astype(jnp.int32)
    prompt_groups = jnp.clip(groups, 0, pieces[0].shape[0] - 1).astype(jnp.int32)

    def page_spec(slot):
        return pl.BlockSpec(
            (1, PAGE_POSITIONS, row_width), lambda r, g, p, c: (p[r * MAXP + slot], 0, 0)
        )

    grid_spec = pltpu.PrefetchScalarGridSpec(
        num_scalar_prefetch=3,
        grid=(count_of_requests,),
        in_specs=[
            pl.BlockSpec((TREE_TOKENS, width), lambda r, g, p, c: (r, 0)),
            pl.BlockSpec((TREE_TOKENS, row_width), lambda r, g, p, c: (r, 0)),
            pl.BlockSpec((1, TREE_TOKENS, TREE_TOKENS), lambda r, g, p, c: (r, 0, 0)),
        ]
        + [pl.BlockSpec((1, part.shape[1], row_width), lambda r, g, p, c: (g[r], 0, 0)) for part in pieces]
        + [page_spec(slot) for slot in range(MAXP)],
        out_specs=pl.BlockSpec((TREE_TOKENS, width), lambda r, g, p, c: (r, 0)),
    )
    return pl.pallas_call(
        attention_kernel,
        grid_spec=grid_spec,
        out_shape=jax.ShapeDtypeStruct((count_of_tokens, width), jnp.bfloat16),
    )(prompt_groups, flat_pages, cache_len.astype(jnp.int32), queries, draft_kv, visible, *pieces, *([cache_page_store] * MAXP))


def run_experts(rows, row_gate, w_in, w_down):
    both = jnp.einsum("td,edf->etf", rows, w_in, preferred_element_type=jnp.float32)
    act = (jax.nn.silu(both[..., :FF]) * both[..., FF:]).astype(jnp.bfloat16)
    result = jnp.einsum("etf,efd->etd", act, w_down, preferred_element_type=jnp.float32).astype(jnp.bfloat16)
    return jnp.sum(jnp.transpose(row_gate)[..., None] * result.astype(jnp.float32), 0)


def exchange_experts(normed, gate, w_in, w_down):
    devices = lax.axis_size("exp")
    count_of_tokens, width = normed.shape
    if devices % 2 != 0:
        rows = lax.all_gather(normed, "exp", axis=0, tiled=True)
        partial = run_experts(rows, gate, w_in, w_down)
        return lax.psum_scatter(partial.astype(jnp.bfloat16), "exp", scatter_dimension=0, tiled=True).astype(jnp.float32)
    half = devices // 2
    me = lax.axis_index("exp")
    core = me % 2
    chip = me // 2

    def chip_shift(x, shift):
        pairs = [(2 * c + b, 2 * ((c + shift) % half) + b) for c in range(half) for b in range(2)]
        return lax.ppermute(x, "exp", pairs)

    def sibling(x):
        return lax.ppermute(x, "exp", [(i, i ^ 1) for i in range(devices)])

    gate_blocks = gate.reshape(devices, count_of_tokens, -1)

    def block_gate(device):
        return lax.dynamic_index_in_dim(gate_blocks, device, 0, keepdims=False)

    same_core = [normed] + [chip_shift(normed, d) for d in range(1, half)]
    other_core = [sibling(rows) for rows in same_core]
    total = None
    for d in range(half):
        source_chip = (chip - d) % half
        paired = run_experts(
            jnp.concatenate([same_core[d], other_core[d]], 0),
            jnp.concatenate([block_gate(2 * source_chip + core), block_gate(2 * source_chip + 1 - core)], 0),
            w_in,
            w_down,
        )
        same_partial = paired[:count_of_tokens]
        other_partial = paired[count_of_tokens:]
        merged = same_partial + sibling(other_partial.astype(jnp.bfloat16)).astype(jnp.float32)
        if d == 0:
            total = merged if total is None else total + merged
        else:
            arrived = chip_shift(merged.astype(jnp.bfloat16), -d).astype(jnp.float32)
            total = arrived if total is None else total + arrived
    return total


def per_device(
    resid,
    queries,
    draft_kv,
    prompt_key_value,
    cache_page_store,
    page_table,
    cache_len,
    parents,
    groups,
    w_out,
    norm_gain,
    routes,
    route_weight,
    w_in,
    w_down,
):
    local_experts = w_in.shape[0]
    exp_devices = lax.axis_size("exp")
    experts_all = local_experts * exp_devices
    count_of_tokens = routes.shape[0]
    every_expert = jnp.arange(experts_all, dtype=jnp.int32)
    gate_local = jnp.sum(
        jnp.where(routes[:, :, None] == every_expert[None, None, :], route_weight[:, :, None], jnp.float32(0.0)),
        1,
    )
    gate_gathered = lax.all_gather(gate_local, "exp", axis=0, tiled=True)
    gate = lax.dynamic_slice_in_dim(gate_gathered, lax.axis_index("exp") * local_experts, local_experts, 1)
    columns = lax.axis_size("req")
    pieces = [prompt_key_value] + [
        lax.ppermute(prompt_key_value, "req", [(s, (s + d) % columns) for s in range(columns)])
        for d in range(1, columns)
    ]
    gate, pieces = lax.optimization_barrier((gate, pieces))
    attended = attend(queries, draft_kv, pieces, cache_page_store, page_table, cache_len, parents, groups)
    mixed = resid.astype(jnp.float32) + jnp.dot(attended, w_out, preferred_element_type=jnp.float32)
    spread = jnp.mean(mixed * mixed, -1, keepdims=True)
    normed = (mixed * lax.rsqrt(spread + 1e-05) * norm_gain).astype(jnp.bfloat16)
    blended = exchange_experts(normed, gate, w_in, w_down)
    return (mixed + blended).astype(jnp.bfloat16)


def solution(mesh):
    in_specs = (
        P(("req", "exp"), None),
        P(("req", "exp"), None),
        P(("req", "exp"), None),
        P("exp", "req", None),
        P(("req", "exp"), None, None),
        P(("req", "exp"), None),
        P(("req", "exp")),
        P(("req", "exp"), None),
        P(("req", "exp")),
        P(),
        P(),
        P(("req", "exp"), None),
        P(("req", "exp"), None),
        P("exp", None, None),
        P("exp", None, None),
    )
    out_specs = P(("req", "exp"), None)
    return jax.shard_map(
        per_device, mesh=mesh, in_specs=in_specs, out_specs=out_specs, check_vma=False
    )
```

```python
import math

import jax
import jax.numpy as jnp
from jax import lax
from jax.experimental import pallas as pl
from jax.experimental.pallas import tpu as pltpu
from jax.sharding import PartitionSpec as P

D = 1536
QUERY_HEADS = 24
KEY_VALUE_HEADS = 8
HEAD_WIDTH = 64
FF = 512
TOPK = 8
TREE_TOKENS = 32
GROUPS_PER_COLUMN = 2
PAGE_POSITIONS = 64
MAXP = 6


def ancestry(parent_rows):
    tree_size = parent_rows.shape[1]
    positions = jnp.arange(tree_size, dtype=jnp.int32)
    linked = (parent_rows[:, :, None] == positions[None, None, :]).astype(jnp.float32)
    reach = jnp.eye(tree_size, dtype=jnp.float32)[None] + linked
    for sweep in range((tree_size - 1).bit_length()):
        reach = jnp.minimum(
            jnp.einsum("bij,bjk->bik", reach, reach, precision=lax.Precision.HIGHEST),
            jnp.float32(1.0),
        )
    return reach > 0.5


def attention_kernel(groups_ref, pages_ref, lengths_ref, queries_ref, tree_ref, visible_ref, *rest):
    prompt_refs = rest[: len(rest) - MAXP - 1]
    page_refs = rest[len(prompt_refs) : len(prompt_refs) + MAXP]
    out_ref = rest[-1]
    request = pl.program_id(0)
    key_value_width = KEY_VALUE_HEADS * HEAD_WIDTH
    heads_repeated = QUERY_HEADS // KEY_VALUE_HEADS
    rows = heads_repeated * TREE_TOKENS
    scale_factor = HEAD_WIDTH ** (-0.5)
    tree_visible = jnp.concatenate([visible_ref[0]] * heads_repeated, 0) > 0.5
    positions = lax.broadcasted_iota(jnp.int32, (rows, MAXP * PAGE_POSITIONS), 1)
    cache_visible = positions < lengths_ref[request]
    contract = (((1,), (1,)), ((), ()))

    for kv in range(KEY_VALUE_HEADS):
        key_at = kv * HEAD_WIDTH
        value_at = key_value_width + kv * HEAD_WIDTH
        query_rows = jnp.concatenate(
            [
                queries_ref[:, (kv * heads_repeated + j) * HEAD_WIDTH : (kv * heads_repeated + j + 1) * HEAD_WIDTH]
                for j in range(heads_repeated)
            ],
            0,
        )
        prompt_keys = jnp.concatenate([p[0, :, key_at : key_at + HEAD_WIDTH] for p in prompt_refs], 0)
        prompt_values = jnp.concatenate([p[0, :, value_at : value_at + HEAD_WIDTH] for p in prompt_refs], 0)
        cache_keys = jnp.concatenate([p[0, :, key_at : key_at + HEAD_WIDTH] for p in page_refs], 0)
        cache_values = jnp.concatenate([p[0, :, value_at : value_at + HEAD_WIDTH] for p in page_refs], 0)
        tree_keys = tree_ref[:, key_at : key_at + HEAD_WIDTH]
        tree_values = tree_ref[:, value_at : value_at + HEAD_WIDTH]
        prompt_scores = lax.dot_general(query_rows, prompt_keys, contract, preferred_element_type=jnp.float32) * scale_factor
        cache_scores = lax.dot_general(query_rows, cache_keys, contract, preferred_element_type=jnp.float32) * scale_factor
        tree_scores = lax.dot_general(query_rows, tree_keys, contract, preferred_element_type=jnp.float32) * scale_factor
        cache_scores = jnp.where(cache_visible, cache_scores, -jnp.inf)
        tree_scores = jnp.where(tree_visible, tree_scores, -jnp.inf)
        peak = jnp.maximum(
            jnp.maximum(jnp.max(prompt_scores, -1, keepdims=True), jnp.max(cache_scores, -1, keepdims=True)),
            jnp.max(tree_scores, -1, keepdims=True),
        )
        prompt_exp = jnp.exp(prompt_scores - peak)
        cache_exp = jnp.exp(cache_scores - peak)
        tree_exp = jnp.exp(tree_scores - peak)
        denom = (
            jnp.sum(prompt_exp, -1, keepdims=True)
            + jnp.sum(cache_exp, -1, keepdims=True)
            + jnp.sum(tree_exp, -1, keepdims=True)
        )
        numer = (
            jnp.dot(prompt_exp.astype(jnp.bfloat16), prompt_values, preferred_element_type=jnp.float32)
            + jnp.dot(cache_exp.astype(jnp.bfloat16), cache_values, preferred_element_type=jnp.float32)
            + jnp.dot(tree_exp.astype(jnp.bfloat16), tree_values, preferred_element_type=jnp.float32)
        )
        result = (numer / denom).astype(jnp.bfloat16)
        for j in range(heads_repeated):
            head = kv * heads_repeated + j
            out_ref[:, head * HEAD_WIDTH : (head + 1) * HEAD_WIDTH] = result[j * TREE_TOKENS : (j + 1) * TREE_TOKENS]


def attend(queries, draft_kv, pieces, cache_page_store, page_table, cache_len, parents, groups):
    count_of_tokens, width = queries.shape
    count_of_requests = page_table.shape[0]
    row_width = draft_kv.shape[1]
    store_pages = cache_page_store.shape[0]
    visible = ancestry(parents).astype(jnp.float32)
    flat_pages = jnp.clip(page_table.reshape(-1), 0, store_pages - 1).astype(jnp.int32)
    prompt_groups = jnp.clip(groups, 0, pieces[0].shape[0] - 1).astype(jnp.int32)

    def page_spec(slot):
        return pl.BlockSpec(
            (1, PAGE_POSITIONS, row_width), lambda r, g, p, c: (p[r * MAXP + slot], 0, 0)
        )

    grid_spec = pltpu.PrefetchScalarGridSpec(
        num_scalar_prefetch=3,
        grid=(count_of_requests,),
        in_specs=[
            pl.BlockSpec((TREE_TOKENS, width), lambda r, g, p, c: (r, 0)),
            pl.BlockSpec((TREE_TOKENS, row_width), lambda r, g, p, c: (r, 0)),
            pl.BlockSpec((1, TREE_TOKENS, TREE_TOKENS), lambda r, g, p, c: (r, 0, 0)),
        ]
        + [pl.BlockSpec((1, part.shape[1], row_width), lambda r, g, p, c: (g[r], 0, 0)) for part in pieces]
        + [page_spec(slot) for slot in range(MAXP)],
        out_specs=pl.BlockSpec((TREE_TOKENS, width), lambda r, g, p, c: (r, 0)),
    )
    return pl.pallas_call(
        attention_kernel,
        grid_spec=grid_spec,
        out_shape=jax.ShapeDtypeStruct((count_of_tokens, width), jnp.bfloat16),
    )(prompt_groups, flat_pages, cache_len.astype(jnp.int32), queries, draft_kv, visible, *pieces, *([cache_page_store] * MAXP))


def run_experts(rows, row_gate, w_in, w_down):
    both = jnp.einsum("td,edf->etf", rows, w_in, preferred_element_type=jnp.float32)
    act = (jax.nn.silu(both[..., :FF]) * both[..., FF:]).astype(jnp.bfloat16)
    result = jnp.einsum("etf,efd->etd", act, w_down, preferred_element_type=jnp.float32).astype(jnp.bfloat16)
    return jnp.sum(jnp.transpose(row_gate)[..., None] * result.astype(jnp.float32), 0)


def exchange_experts(normed, gate, w_in, w_down):
    devices = lax.axis_size("exp")
    count_of_tokens, width = normed.shape
    if devices % 2 != 0:
        rows = lax.all_gather(normed, "exp", axis=0, tiled=True)
        partial = run_experts(rows, gate, w_in, w_down)
        return lax.psum_scatter(partial.astype(jnp.bfloat16), "exp", scatter_dimension=0, tiled=True).astype(jnp.float32)
    half = devices // 2
    me = lax.axis_index("exp")
    core = me % 2
    chip = me // 2

    def chip_shift(x, shift):
        pairs = [(2 * c + b, 2 * ((c + shift) % half) + b) for c in range(half) for b in range(2)]
        return lax.ppermute(x, "exp", pairs)

    def sibling(x):
        return lax.ppermute(x, "exp", [(i, i ^ 1) for i in range(devices)])

    gate_blocks = gate.reshape(devices, count_of_tokens, -1)

    def block_gate(device):
        return lax.dynamic_index_in_dim(gate_blocks, device, 0, keepdims=False)

    order = [0] + sorted(range(1, half), key=lambda d: -min(d, half - d))
    same_core = {d: normed if d == 0 else chip_shift(normed, d) for d in order}
    other_core = {d: sibling(same_core[d]) for d in order}
    total = None
    for d in order:
        source_chip = (chip - d) % half
        other_partial = run_experts(other_core[d], block_gate(2 * source_chip + 1 - core), w_in, w_down)
        same_partial = run_experts(same_core[d], block_gate(2 * source_chip + core), w_in, w_down)
        merged = same_partial + sibling(other_partial.astype(jnp.bfloat16)).astype(jnp.float32)
        if d == 0:
            total = merged if total is None else total + merged
        else:
            arrived = chip_shift(merged.astype(jnp.bfloat16), -d).astype(jnp.float32)
            total = arrived if total is None else total + arrived
    return total


def per_device(
    resid,
    queries,
    draft_kv,
    prompt_key_value,
    cache_page_store,
    page_table,
    cache_len,
    parents,
    groups,
    w_out,
    norm_gain,
    routes,
    route_weight,
    w_in,
    w_down,
):
    local_experts = w_in.shape[0]
    exp_devices = lax.axis_size("exp")
    experts_all = local_experts * exp_devices
    count_of_tokens = routes.shape[0]
    every_expert = jnp.arange(experts_all, dtype=jnp.int32)
    gate_local = jnp.sum(
        jnp.where(routes[:, :, None] == every_expert[None, None, :], route_weight[:, :, None], jnp.float32(0.0)),
        1,
    )
    gate_gathered = lax.all_gather(gate_local, "exp", axis=0, tiled=True)
    gate = lax.dynamic_slice_in_dim(gate_gathered, lax.axis_index("exp") * local_experts, local_experts, 1)
    columns = lax.axis_size("req")
    pieces = [prompt_key_value] + [
        lax.ppermute(prompt_key_value, "req", [(s, (s + d) % columns) for s in range(columns)])
        for d in range(1, columns)
    ]
    gate, pieces = lax.optimization_barrier((gate, pieces))
    attended = attend(queries, draft_kv, pieces, cache_page_store, page_table, cache_len, parents, groups)
    mixed = resid.astype(jnp.float32) + jnp.dot(attended, w_out, preferred_element_type=jnp.float32)
    spread = jnp.mean(mixed * mixed, -1, keepdims=True)
    normed = (mixed * lax.rsqrt(spread + 1e-05) * norm_gain).astype(jnp.bfloat16)
    blended = exchange_experts(normed, gate, w_in, w_down)
    return (mixed + blended).astype(jnp.bfloat16)


def solution(mesh):
    in_specs = (
        P(("req", "exp"), None),
        P(("req", "exp"), None),
        P(("req", "exp"), None),
        P("exp", "req", None),
        P(("req", "exp"), None, None),
        P(("req", "exp"), None),
        P(("req", "exp")),
        P(("req", "exp"), None),
        P(("req", "exp")),
        P(),
        P(),
        P(("req", "exp"), None),
        P(("req", "exp"), None),
        P("exp", None, None),
        P("exp", None, None),
    )
    out_specs = P(("req", "exp"), None)
    return jax.shard_map(
        per_device, mesh=mesh, in_specs=in_specs, out_specs=out_specs, check_vma=False
    )
```

```python
import math

import jax
import jax.numpy as jnp
from jax import lax
from jax.experimental import pallas as pl
from jax.experimental.pallas import tpu as pltpu
from jax.sharding import PartitionSpec as P

D = 1536
QUERY_HEADS = 24
KEY_VALUE_HEADS = 8
HEAD_WIDTH = 64
FF = 512
TOPK = 8
TREE_TOKENS = 32
GROUPS_PER_COLUMN = 2
PAGE_POSITIONS = 64
MAXP = 6


def ancestry(parent_rows):
    tree_size = parent_rows.shape[1]
    positions = jnp.arange(tree_size, dtype=jnp.int32)
    linked = (parent_rows[:, :, None] == positions[None, None, :]).astype(jnp.float32)
    reach = jnp.eye(tree_size, dtype=jnp.float32)[None] + linked
    for sweep in range((tree_size - 1).bit_length()):
        reach = jnp.minimum(
            jnp.einsum("bij,bjk->bik", reach, reach, precision=lax.Precision.HIGHEST),
            jnp.float32(1.0),
        )
    return reach > 0.5


def attention_kernel(groups_ref, pages_ref, lengths_ref, queries_ref, tree_ref, visible_ref, *rest):
    prompt_refs = rest[: len(rest) - MAXP - 1]
    page_refs = rest[len(prompt_refs) : len(prompt_refs) + MAXP]
    out_ref = rest[-1]
    request = pl.program_id(0)
    key_value_width = KEY_VALUE_HEADS * HEAD_WIDTH
    heads_repeated = QUERY_HEADS // KEY_VALUE_HEADS
    rows = heads_repeated * TREE_TOKENS
    scale_factor = HEAD_WIDTH ** (-0.5)
    tree_visible = jnp.concatenate([visible_ref[0]] * heads_repeated, 0) > 0.5
    positions = lax.broadcasted_iota(jnp.int32, (rows, MAXP * PAGE_POSITIONS), 1)
    cache_visible = positions < lengths_ref[request]
    contract = (((1,), (1,)), ((), ()))

    for kv in range(KEY_VALUE_HEADS):
        key_at = kv * HEAD_WIDTH
        value_at = key_value_width + kv * HEAD_WIDTH
        query_rows = jnp.concatenate(
            [
                queries_ref[:, (kv * heads_repeated + j) * HEAD_WIDTH : (kv * heads_repeated + j + 1) * HEAD_WIDTH]
                for j in range(heads_repeated)
            ],
            0,
        )
        prompt_keys = jnp.concatenate([p[0, :, key_at : key_at + HEAD_WIDTH] for p in prompt_refs], 0)
        prompt_values = jnp.concatenate([p[0, :, value_at : value_at + HEAD_WIDTH] for p in prompt_refs], 0)
        cache_keys = jnp.concatenate([p[0, :, key_at : key_at + HEAD_WIDTH] for p in page_refs], 0)
        cache_values = jnp.concatenate([p[0, :, value_at : value_at + HEAD_WIDTH] for p in page_refs], 0)
        tree_keys = tree_ref[:, key_at : key_at + HEAD_WIDTH]
        tree_values = tree_ref[:, value_at : value_at + HEAD_WIDTH]
        prompt_scores = lax.dot_general(query_rows, prompt_keys, contract, preferred_element_type=jnp.float32) * scale_factor
        cache_scores = lax.dot_general(query_rows, cache_keys, contract, preferred_element_type=jnp.float32) * scale_factor
        tree_scores = lax.dot_general(query_rows, tree_keys, contract, preferred_element_type=jnp.float32) * scale_factor
        cache_scores = jnp.where(cache_visible, cache_scores, -jnp.inf)
        tree_scores = jnp.where(tree_visible, tree_scores, -jnp.inf)
        peak = jnp.maximum(
            jnp.maximum(jnp.max(prompt_scores, -1, keepdims=True), jnp.max(cache_scores, -1, keepdims=True)),
            jnp.max(tree_scores, -1, keepdims=True),
        )
        prompt_exp = jnp.exp(prompt_scores - peak)
        cache_exp = jnp.exp(cache_scores - peak)
        tree_exp = jnp.exp(tree_scores - peak)
        denom = (
            jnp.sum(prompt_exp, -1, keepdims=True)
            + jnp.sum(cache_exp, -1, keepdims=True)
            + jnp.sum(tree_exp, -1, keepdims=True)
        )
        numer = (
            jnp.dot(prompt_exp.astype(jnp.bfloat16), prompt_values, preferred_element_type=jnp.float32)
            + jnp.dot(cache_exp.astype(jnp.bfloat16), cache_values, preferred_element_type=jnp.float32)
            + jnp.dot(tree_exp.astype(jnp.bfloat16), tree_values, preferred_element_type=jnp.float32)
        )
        result = (numer / denom).astype(jnp.bfloat16)
        for j in range(heads_repeated):
            head = kv * heads_repeated + j
            out_ref[:, head * HEAD_WIDTH : (head + 1) * HEAD_WIDTH] = result[j * TREE_TOKENS : (j + 1) * TREE_TOKENS]


def attend(queries, draft_kv, pieces, cache_page_store, page_table, cache_len, parents, groups):
    count_of_tokens, width = queries.shape
    count_of_requests = page_table.shape[0]
    row_width = draft_kv.shape[1]
    store_pages = cache_page_store.shape[0]
    visible = ancestry(parents).astype(jnp.float32)
    flat_pages = jnp.clip(page_table.reshape(-1), 0, store_pages - 1).astype(jnp.int32)
    prompt_groups = jnp.clip(groups, 0, pieces[0].shape[0] - 1).astype(jnp.int32)

    def page_spec(slot):
        return pl.BlockSpec(
            (1, PAGE_POSITIONS, row_width), lambda r, g, p, c: (p[r * MAXP + slot], 0, 0)
        )

    grid_spec = pltpu.PrefetchScalarGridSpec(
        num_scalar_prefetch=3,
        grid=(count_of_requests,),
        in_specs=[
            pl.BlockSpec((TREE_TOKENS, width), lambda r, g, p, c: (r, 0)),
            pl.BlockSpec((TREE_TOKENS, row_width), lambda r, g, p, c: (r, 0)),
            pl.BlockSpec((1, TREE_TOKENS, TREE_TOKENS), lambda r, g, p, c: (r, 0, 0)),
        ]
        + [pl.BlockSpec((1, part.shape[1], row_width), lambda r, g, p, c: (g[r], 0, 0)) for part in pieces]
        + [page_spec(slot) for slot in range(MAXP)],
        out_specs=pl.BlockSpec((TREE_TOKENS, width), lambda r, g, p, c: (r, 0)),
    )
    return pl.pallas_call(
        attention_kernel,
        grid_spec=grid_spec,
        out_shape=jax.ShapeDtypeStruct((count_of_tokens, width), jnp.bfloat16),
    )(prompt_groups, flat_pages, cache_len.astype(jnp.int32), queries, draft_kv, visible, *pieces, *([cache_page_store] * MAXP))


def run_experts(rows, row_gate, w_in, w_down):
    both = jnp.einsum("td,edf->etf", rows, w_in, preferred_element_type=jnp.float32)
    act = (jax.nn.silu(both[..., :FF]) * both[..., FF:]).astype(jnp.bfloat16)
    result = jnp.einsum("etf,efd->etd", act, w_down, preferred_element_type=jnp.float32).astype(jnp.bfloat16)
    return jnp.sum(jnp.transpose(row_gate)[..., None] * result.astype(jnp.float32), 0)


def exchange_experts(normed, gate, w_in, w_down):
    devices = lax.axis_size("exp")
    count_of_tokens, width = normed.shape
    if devices % 2 != 0:
        rows = lax.all_gather(normed, "exp", axis=0, tiled=True)
        partial = run_experts(rows, gate, w_in, w_down)
        return lax.psum_scatter(partial.astype(jnp.bfloat16), "exp", scatter_dimension=0, tiled=True).astype(jnp.float32)
    half = devices // 2
    me = lax.axis_index("exp")
    core = me % 2
    chip = me // 2

    def chip_shift(x, shift):
        pairs = [(2 * c + b, 2 * ((c + shift) % half) + b) for c in range(half) for b in range(2)]
        return lax.ppermute(x, "exp", pairs)

    def sibling(x):
        return lax.ppermute(x, "exp", [(i, i ^ 1) for i in range(devices)])

    gate_blocks = gate.reshape(devices, count_of_tokens, -1)

    def block_gate(device):
        return lax.dynamic_index_in_dim(gate_blocks, device, 0, keepdims=False)

    same_core = [normed] + [chip_shift(normed, d) for d in range(1, half)]
    other_core = [sibling(rows) for rows in same_core]
    total = None
    for d in range(half):
        source_chip = (chip - d) % half
        other_partial = run_experts(other_core[d], block_gate(2 * source_chip + 1 - core), w_in, w_down)
        same_partial = run_experts(same_core[d], block_gate(2 * source_chip + core), w_in, w_down)
        merged = same_partial + sibling(other_partial.astype(jnp.bfloat16)).astype(jnp.float32)
        if d == 0:
            total = merged if total is None else total + merged
        else:
            arrived = chip_shift(merged.astype(jnp.bfloat16), -d).astype(jnp.float32)
            total = arrived if total is None else total + arrived
    return total


def per_device(
    resid,
    queries,
    draft_kv,
    prompt_key_value,
    cache_page_store,
    page_table,
    cache_len,
    parents,
    groups,
    w_out,
    norm_gain,
    routes,
    route_weight,
    w_in,
    w_down,
):
    local_experts = w_in.shape[0]
    exp_devices = lax.axis_size("exp")
    experts_all = local_experts * exp_devices
    count_of_tokens = routes.shape[0]
    every_expert = jnp.arange(experts_all, dtype=jnp.int32)
    gate_local = jnp.sum(
        jnp.where(routes[:, :, None] == every_expert[None, None, :], route_weight[:, :, None], jnp.float32(0.0)),
        1,
    )
    gate_gathered = lax.all_gather(gate_local, "exp", axis=0, tiled=True)
    gate = lax.dynamic_slice_in_dim(gate_gathered, lax.axis_index("exp") * local_experts, local_experts, 1)
    columns = lax.axis_size("req")
    def shifted(x, d):
        return lax.ppermute(x, "req", [(s, (s + d) % columns) for s in range(columns)])

    if columns == 4 and prompt_key_value.shape[0] == 2:
        forward = shifted(prompt_key_value, 1)
        backward = shifted(prompt_key_value, columns - 1)
        across = jnp.concatenate([shifted(forward[0:1], 1), shifted(backward[1:2], columns - 1)], 0)
        pieces = [prompt_key_value, forward, across, backward]
    else:
        pieces = [prompt_key_value] + [shifted(prompt_key_value, d) for d in range(1, columns)]
    gate, pieces = lax.optimization_barrier((gate, pieces))
    attended = attend(queries, draft_kv, pieces, cache_page_store, page_table, cache_len, parents, groups)
    mixed = resid.astype(jnp.float32) + jnp.dot(attended, w_out, preferred_element_type=jnp.float32)
    spread = jnp.mean(mixed * mixed, -1, keepdims=True)
    normed = (mixed * lax.rsqrt(spread + 1e-05) * norm_gain).astype(jnp.bfloat16)
    blended = exchange_experts(normed, gate, w_in, w_down)
    return (mixed + blended).astype(jnp.bfloat16)


def solution(mesh):
    in_specs = (
        P(("req", "exp"), None),
        P(("req", "exp"), None),
        P(("req", "exp"), None),
        P("exp", "req", None),
        P(("req", "exp"), None, None),
        P(("req", "exp"), None),
        P(("req", "exp")),
        P(("req", "exp"), None),
        P(("req", "exp")),
        P(),
        P(),
        P(("req", "exp"), None),
        P(("req", "exp"), None),
        P("exp", None, None),
        P("exp", None, None),
    )
    out_specs = P(("req", "exp"), None)
    return jax.shard_map(
        per_device, mesh=mesh, in_specs=in_specs, out_specs=out_specs, check_vma=False
    )
```
